512 devices in a mesh: gx: 16 (over y, core), gy: 32 (over x, z).
Axes of the slice: x: 4, y: 8, z: 8, core: 2. Of those that a mesh axis runs over, the one named last changes fastest.
Arguments:
- adjoint_in: float32 [19, 4, 256, 4096], P(None, None, 'gx', 'gy'), may hold values from -6 to 6
- forward_pops: bfloat16 [2, 19, 4, 256, 4096], P(None, None, None, 'gx', 'gy'), may hold values from 0 to 0.42, as said below
- solid_mask: int32 [4, 256, 4096], P(None, 'gx', 'gy'), may hold values 0 or 1
- region_label: int32 [256, 4096], P('gx', 'gy'), may hold values from 0 to 2
- design: float32 [256, 4096], P('gx', 'gy'), may hold values from 0 to 1
Outputs:
- adjoint_out: float32 [19, 4, 256, 4096], P(None, None, 'gx', 'gy')
- sensitivity: float32 [256, 4096], P('gx', 'gy')
The draws below stay inside these ranges and needn't reach their ends.
Inputs may be any that keep to these rules, and one draw needn't show every extreme that they name: `forward_pops`: each population lies between 0.75 and 1.25 times its lattice weight.
All inputs are finite; a program needn't handle non-finite values. No bound on the sum of `solid_mask` on one device may be relied on, other than what follows from the above.
Results may differ from the reference program's by a relative error of at most 0.0004.
Values sent between devices are 32-bit elements; how exact they have to be, the bound alone decides.
No kernel may reach another device: no remote copies, remote signals or barrier semaphores. Data moves between devices by JAX's collectives and lax.ppermute only.
A program may use at most 128 MiB of HBM per device.

```python
import jax
import jax.numpy as jnp
from jax import lax

NZ = 4
SWEEPS = 4
NX = 256
NY = 4096


def draw_forward_pops(key, part):
    weights = jnp.asarray([1.0 / 3.0] + [1.0 / 18.0] * 6 + [1.0 / 36.0] * 12, jnp.float32).reshape(1, 19, 1, 1, 1)
    shape_all = (2, 19, NZ, NX, NY)
    factor = 1.0 + 0.1 * jnp.clip(jax.random.normal(key, shape_all, jnp.float32), -2.5, 2.5)
    return (weights * factor).astype(jnp.bfloat16)


def touch_ends(values, key, low, high):
    spot = [jax.random.randint(jax.random.fold_in(key, axis), (), 0, length) for axis, length in enumerate(values.shape)]
    widest = values.shape.index(max(values.shape))
    neighbour = spot[:widest] + [(spot[widest] + 1) % values.shape[widest]] + spot[widest + 1:]
    return values.at[tuple(spot)].set(low).at[tuple(neighbour)].set(high)


def block_levels(own_key, dims, cuts, smallest, top_value):
    gain, own = 1.0, jax.random.fold_in(own_key, 6)
    for position, shards_of in cuts:
        draws = jnp.exp(jax.random.uniform(jax.random.fold_in(own, position), (shards_of,), jnp.float32, smallest / len(cuts), top_value / len(cuts)))
        gain = gain * jnp.repeat(draws, dims[position] // shards_of).reshape([-1 if axis == position else 1 for axis in range(len(dims))])
    return gain


def bell_draw(own_key, extent, width, bound, shards=(), held_as=jnp.bfloat16):
    array = width * jax.random.normal(own_key, extent, jnp.float32)
    if shards:
        array = array * block_levels(own_key, extent, shards, -0.22, 0.18)
    return jnp.clip(array, -bound, bound).astype(held_as)


def setup_inputs(seed: int = 0) -> dict:
    key_list = jax.random.split(jax.random.key(seed), 6)
    return {
        "adjoint_in": bell_draw(key_list[0], (19, NZ, NX, NY), 1.0, 6.0, ((2, 16), (3, 32)), jnp.float32),
        "forward_pops": draw_forward_pops(jax.random.fold_in(key_list[5], 71), 0),
        "solid_mask": touch_ends((jax.random.randint(key_list[2], (NZ, NX, NY), 0, 6) < 1).astype(jnp.int32), jax.random.fold_in(key_list[2], 1), 0, 1),
        "region_label": touch_ends(jax.random.randint(key_list[3], (NX, NY), 0, 3), jax.random.fold_in(key_list[3], 1), 0, 2).astype(jnp.int32),
        "design": jnp.clip(1.0 * jax.random.uniform(key_list[4], (NX, NY), jnp.float32) ** block_levels(key_list[4], (NX, NY), ((0, 16), (1, 32)), -0.2, 0.2), 0.0, 1.0),
    }


VELOCITIES = [(0, 0, 0), (1, 0, 0), (-1, 0, 0), (0, 1, 0), (0, -1, 0), (0, 0, 1), (0, 0, -1), (1, 1, 0), (-1, -1, 0), (1, -1, 0), (-1, 1, 0), (1, 0, 1), (-1, 0, -1), (1, 0, -1), (-1, 0, 1), (0, 1, 1), (0, -1, -1), (0, 1, -1), (0, -1, 1)]
OPPOSITE = [0, 2, 1, 4, 3, 6, 5, 8, 7, 10, 9, 12, 11, 14, 13, 16, 15, 18, 17]
WEIGHTS = [1.0 / 3.0] + [1.0 / 18.0] * 6 + [1.0 / 36.0] * 12
RELAX_RATES = [0.0] * 4 + [1.6] * 6 + [1.4] * 6 + [1.2] * 3
EXPONENTS = [(0, 0, 0), (1, 0, 0), (0, 1, 0), (0, 0, 1), (2, 0, 0), (0, 2, 0), (0, 0, 2), (1, 1, 0), (1, 0, 1), (0, 1, 1), (2, 1, 0), (2, 0, 1), (1, 2, 0), (0, 2, 1), (1, 0, 2), (0, 1, 2), (2, 2, 0), (2, 0, 2), (0, 2, 2)]
BLOCK_LIMIT = 0.5
SENSE_SCALE = 20.0
FILTER_WEIGHT = 16.0

def moment_table():
    rows_out = []
    for expo in EXPONENTS:
        vector = [float(vel[0] ** expo[0] * vel[1] ** expo[1] * vel[2] ** expo[2]) for vel in VELOCITIES]
        for prior in rows_out:
            factor = sum((a * b for a, b in zip(vector, prior))) / sum((b * b for b in prior))
            vector = [a - factor * b for a, b in zip(vector, prior)]
        rows_out.append(vector)
    norms = [sum((b * b for b in row)) for row in rows_out]
    table = []
    for first in range(19):
        line = []
        for second in range(19):
            line.append(sum((rows_out[k][first] / norms[k] * RELAX_RATES[k] * rows_out[k][second] for k in range(19))))
        table.append(line)
    return table

def collide(popul, blocking):
    relax_matrix = jnp.asarray(moment_table(), jnp.float32)
    veloc = jnp.asarray(VELOCITIES, jnp.float32)
    weights = jnp.asarray(WEIGHTS, jnp.float32)
    density = lax.optimization_barrier(jnp.sum(popul, axis=0))
    momentum = jnp.dot(veloc.T, popul, precision=lax.Precision.HIGHEST)
    velocity = momentum / density
    along_u = jnp.dot(veloc, velocity, precision=lax.Precision.HIGHEST)
    speed_sq = lax.optimization_barrier(jnp.sum(velocity * velocity, axis=0))
    equilib = weights[:, None] * density * (1.0 + 3.0 * along_u + 4.5 * along_u * along_u - 1.5 * speed_sq)
    relaxed = popul - jnp.dot(relax_matrix, popul - equilib, precision=lax.Precision.HIGHEST)
    reflected = popul[jnp.asarray(OPPOSITE, jnp.int32)]
    return ((1.0 - blocking) * relaxed + blocking * reflected, reflected - relaxed)

def adjoint_cell(saved_now, pulled, blocking, lever):

    def forward(popul):
        return collide(popul, blocking)
    _, back_fn, change = jax.vjp(forward, saved_now, has_aux=True)
    result, = back_fn(pulled)
    term = lax.optimization_barrier(jnp.sum(pulled * change, axis=0)) * lever
    return (result, term)

def pull_back(padded, width_x, width_y):
    pieces = []
    for slot in range(19):
        step_x, step_y, step_z = VELOCITIES[slot]
        piece = padded[slot, :, 1 + step_x:1 + step_x + width_x, 1 + step_y:1 + step_y + width_y]
        pieces.append(jnp.roll(piece, -step_z, axis=0))
    return jnp.stack(pieces)

def reference(adjoint_in, forward_pops, solid_mask, region_label, design):
    width_x, width_y = design.shape
    inside = region_label > 0
    blocking = jnp.where(solid_mask == 1, 1.0, jnp.where(inside[None], BLOCK_LIMIT * design[None], 0.0)).astype(jnp.float32)
    lever = jnp.where((solid_mask == 0) & inside[None], BLOCK_LIMIT, 0.0).astype(jnp.float32)
    adjoint = adjoint_in
    raw = jnp.zeros((width_x, width_y), jnp.float32)
    for section in (1, 0):
        padded = jnp.pad(adjoint, ((0, 0), (0, 0), (1, 1), (1, 1)))
        pulled = pull_back(padded, width_x, width_y)
        saved_now = forward_pops[section].astype(jnp.float32)

        def per_plane(items):
            saved_plane, pulled_plane, block_plane, lever_plane = items
            result, term = adjoint_cell(saved_plane.reshape(19, -1), pulled_plane.reshape(19, -1), block_plane.reshape(-1), lever_plane.reshape(-1))
            return (result.reshape(19, width_x, width_y), term.reshape(width_x, width_y))
        results, terms = lax.map(per_plane, (jnp.moveaxis(saved_now, 1, 0), jnp.moveaxis(pulled, 1, 0), blocking, lever))
        adjoint = jnp.moveaxis(results, 0, 1)
        raw = raw + lax.optimization_barrier(jnp.sum(terms, axis=0))
    raw = SENSE_SCALE * raw
    smooth = raw
    for sweep in range(SWEEPS):
        framed = jnp.pad(smooth, 1)
        beside_all = framed[:-2, 1:-1] + framed[2:, 1:-1] + framed[1:-1, :-2] + framed[1:-1, 2:]
        smooth = (raw + FILTER_WEIGHT * beside_all) / (1.0 + 4.0 * FILTER_WEIGHT)
    region_one = (region_label == 1).astype(jnp.float32)
    region_two = (region_label == 2).astype(jnp.float32)
    mean_one = jnp.sum(smooth * region_one) / jnp.maximum(jnp.sum(region_one), 1.0)
    mean_two = jnp.sum(smooth * region_two) / jnp.maximum(jnp.sum(region_two), 1.0)
    sensitivity = region_one * (smooth - mean_one) + region_two * (smooth - mean_two)
    return (adjoint, sensitivity)
```

```python
import jax
import jax.numpy as jnp
from jax import lax
from jax.sharding import PartitionSpec as P

SWEEPS = 4


VELOCITIES = [
    (0, 0, 0),
    (1, 0, 0),
    (-1, 0, 0),
    (0, 1, 0),
    (0, -1, 0),
    (0, 0, 1),
    (0, 0, -1),
    (1, 1, 0),
    (-1, -1, 0),
    (1, -1, 0),
    (-1, 1, 0),
    (1, 0, 1),
    (-1, 0, -1),
    (1, 0, -1),
    (-1, 0, 1),
    (0, 1, 1),
    (0, -1, -1),
    (0, 1, -1),
    (0, -1, 1),
]
OPPOSITE = [0, 2, 1, 4, 3, 6, 5, 8, 7, 10, 9, 12, 11, 14, 13, 16, 15, 18, 17]
WEIGHTS = [1.0 / 3.0] + [1.0 / 18.0] * 6 + [1.0 / 36.0] * 12
RELAX_RATES = [0.0] * 4 + [1.6] * 6 + [1.4] * 6 + [1.2] * 3
EXPONENTS = [
    (0, 0, 0),
    (1, 0, 0),
    (0, 1, 0),
    (0, 0, 1),
    (2, 0, 0),
    (0, 2, 0),
    (0, 0, 2),
    (1, 1, 0),
    (1, 0, 1),
    (0, 1, 1),
    (2, 1, 0),
    (2, 0, 1),
    (1, 2, 0),
    (0, 2, 1),
    (1, 0, 2),
    (0, 1, 2),
    (2, 2, 0),
    (2, 0, 2),
    (0, 2, 2),
]
BLOCK_LIMIT = 0.5
SENSE_SCALE = 20.0
FILTER_WEIGHT = 16.0

import functools

from jax.experimental import pallas as pl
from jax.experimental.pallas import tpu as pltpu

def moment_table():
    rows_out = []
    for expo in EXPONENTS:
        vector = [
            float(vel[0] ** expo[0] * vel[1] ** expo[1] * vel[2] ** expo[2]) for vel in VELOCITIES
        ]
        for prior in rows_out:
            factor = sum((a * b for a, b in zip(vector, prior))) / sum((b * b for b in prior))
            vector = [a - factor * b for a, b in zip(vector, prior)]
        rows_out.append(vector)
    norms = [sum((b * b for b in row)) for row in rows_out]
    table = []
    for first in range(19):
        line = []
        for second in range(19):
            line.append(
                sum(
                    (
                        rows_out[k][first] / norms[k] * RELAX_RATES[k] * rows_out[k][second]
                        for k in range(19)
                    )
                )
            )
        table.append(line)
    return table


RELAX = moment_table()


def neighbour_pairs(dx, dy, nx, ny):
    pairs = []
    for i in range(nx):
        for j in range(ny):
            ti, tj = i + dx, j + dy
            if 0 <= ti < nx and 0 <= tj < ny:
                pairs.append((i * ny + j, ti * ny + tj))
    return pairs


def halo(cells, w):
    nx = lax.axis_size("gx")
    ny = lax.axis_size("gy")
    axes = ("gx", "gy")

    def send(piece, dx, dy):
        return lax.ppermute(piece, axes, neighbour_pairs(dx, dy, nx, ny))

    top = cells[..., :w, :]
    bottom = cells[..., -w:, :]
    left = cells[..., :, :w]
    right = cells[..., :, -w:]
    low_x = send(bottom, 1, 0)
    high_x = send(top, -1, 0)
    low_y = send(right, 0, 1)
    high_y = send(left, 0, -1)
    c_ll = send(cells[..., -w:, -w:], 1, 1)
    c_lh = send(cells[..., -w:, :w], 1, -1)
    c_hl = send(cells[..., :w, -w:], -1, 1)
    c_hh = send(cells[..., :w, :w], -1, -1)
    rows_lo = jnp.concatenate([c_ll, low_x, c_lh], axis=-1)
    rows_mid = jnp.concatenate([low_y, cells, high_y], axis=-1)
    rows_hi = jnp.concatenate([c_hl, high_x, c_hh], axis=-1)
    return jnp.concatenate([rows_lo, rows_mid, rows_hi], axis=-2)


def pull_back(ext, width_x, width_y):
    pieces = []
    for slot in range(19):
        step_x, step_y, step_z = VELOCITIES[slot]
        piece = ext[slot, :, 1 + step_x : 1 + step_x + width_x, 1 + step_y : 1 + step_y + width_y]
        pieces.append(jnp.roll(piece, -step_z, axis=0))
    return jnp.stack(pieces)


def cell_math(g, f, b, lev):
    rho = f[0]
    for i in range(1, 19):
        rho = rho + f[i]
    mom = []
    for d in range(3):
        acc = None
        for i in range(19):
            c = VELOCITIES[i][d]
            if c == 0:
                continue
            acc = (f[i] if acc is None else acc + f[i]) if c > 0 else (-f[i] if acc is None else acc - f[i])
        mom.append(acc)
    u = [m / rho for m in mom]
    usq = u[0] * u[0] + u[1] * u[1] + u[2] * u[2]
    one_b = 1.0 - b
    q = []
    for j in range(19):
        acc = None
        for l in range(19):
            t = RELAX[j][l] * g[l]
            acc = t if acc is None else acc + t
        q.append(acc)
    tsum = None
    for i in range(19):
        cu = None
        for d in range(3):
            c = VELOCITIES[i][d]
            if c == 0:
                continue
            cu = (u[d] if c > 0 else -u[d]) if cu is None else (cu + u[d] if c > 0 else cu - u[d])
        if cu is None:
            phi = 1.0 - 1.5 * usq
        else:
            phi = 1.0 + 3.0 * cu + 4.5 * cu * cu - 1.5 * usq
        eq = WEIGHTS[i] * rho * phi
        t = g[i] * (f[OPPOSITE[i]] - f[i]) + q[i] * (f[i] - eq)
        tsum = t if tsum is None else tsum + t
    term = lev * tsum
    k = [one_b * qj for qj in q]
    wk = [WEIGHTS[i] * k[i] for i in range(19)]
    a_sum = wk[0]
    for i in range(1, 19):
        a_sum = a_sum + wk[i]
    bvec = []
    for d in range(3):
        acc = None
        for i in range(19):
            c = VELOCITIES[i][d]
            if c == 0:
                continue
            acc = (wk[i] if acc is None else acc + wk[i]) if c > 0 else (-wk[i] if acc is None else acc - wk[i])
        bvec.append(acc)
    cmat = {}
    for d in range(3):
        for e in range(d, 3):
            acc = None
            for i in range(19):
                c = VELOCITIES[i][d] * VELOCITIES[i][e]
                if c == 0:
                    continue
                acc = (wk[i] if acc is None else acc + wk[i]) if c > 0 else (-wk[i] if acc is None else acc - wk[i])
            cmat[(d, e)] = acc
            cmat[(e, d)] = acc
    cu_vec = [cmat[(d, 0)] * u[0] + cmat[(d, 1)] * u[1] + cmat[(d, 2)] * u[2] for d in range(3)]
    ucu = u[0] * cu_vec[0] + u[1] * cu_vec[1] + u[2] * cu_vec[2]
    e_val = a_sum - 4.5 * ucu + 1.5 * a_sum * usq
    gvec = [3.0 * bvec[d] + 9.0 * cu_vec[d] - 3.0 * a_sum * u[d] for d in range(3)]
    result = []
    for j in range(19):
        r = one_b * g[j] - k[j] + e_val + b * g[OPPOSITE[j]]
        for d in range(3):
            c = VELOCITIES[j][d]
            if c > 0:
                r = r + gvec[d]
            elif c < 0:
                r = r - gvec[d]
        result.append(r)
    return result, term


def step_kernel(section, rows, g_ref, f_ref, b_ref, l_ref, res_ref, term_ref):
    planes, width_x, _ = b_ref.shape
    chunks = width_x // rows

    def body(idx, acc):
        z = idx // chunks
        x0 = pl.multiple_of((idx % chunks) * rows, rows)
        xs = pl.ds(x0, rows)
        g = [g_ref[i, z, xs, :] for i in range(19)]
        f = [f_ref[section, i, z, xs, :].astype(jnp.float32) for i in range(19)]
        b = b_ref[z, xs, :]
        lev = l_ref[z, xs, :]
        result, term = cell_math(g, f, b, lev)
        for j in range(19):
            res_ref[j, z, xs, :] = result[j]
        term_ref[xs, :] = term_ref[xs, :] + term
        return acc

    term_ref[...] = jnp.zeros_like(term_ref)
    lax.fori_loop(0, planes * chunks, body, 0)


def adjoint_step(section, pulled, forward_pops, blocking, lever):
    _, planes, width_x, width_y = pulled.shape
    rows = 8 if width_x % 8 == 0 else width_x
    vmem = pl.BlockSpec(memory_space=pltpu.VMEM)
    return pl.pallas_call(
        functools.partial(step_kernel, section, rows),
        out_shape=(
            jax.ShapeDtypeStruct(pulled.shape, jnp.float32),
            jax.ShapeDtypeStruct((width_x, width_y), jnp.float32),
        ),
        in_specs=[vmem] * 4,
        out_specs=(vmem, vmem),
    )(pulled, forward_pops, blocking, lever)


def helmholtz(raw, w):
    scale_den = 1.0 + 4.0 * FILTER_WEIGHT
    width_x, width_y = raw.shape
    nx = lax.axis_size("gx")
    ny = lax.axis_size("gy")
    gxi = lax.axis_index("gx")
    gyi = lax.axis_index("gy")
    raw_ext = halo(raw, w)
    xs = gxi * width_x - w + lax.broadcasted_iota(jnp.int32, raw_ext.shape, 0)
    ys = gyi * width_y - w + lax.broadcasted_iota(jnp.int32, raw_ext.shape, 1)
    valid = (xs >= 0) & (xs < nx * width_x) & (ys >= 0) & (ys < ny * width_y)
    smooth = raw_ext
    for sweep in range(SWEEPS):
        framed = jnp.pad(smooth, 1)
        beside_all = framed[:-2, 1:-1] + framed[2:, 1:-1] + framed[1:-1, :-2] + framed[1:-1, 2:]
        smooth = jnp.where(valid, (raw_ext + FILTER_WEIGHT * beside_all) / scale_den, 0.0)
    return smooth[w:-w, w:-w]


def per_device(adjoint_in, forward_pops, solid_mask, region_label, design):
    planes, width_x, width_y = solid_mask.shape
    inside = region_label > 0
    blocking = jnp.where(
        solid_mask == 1, 1.0, jnp.where(inside[None], BLOCK_LIMIT * design[None], 0.0)
    ).astype(jnp.float32)
    lever = jnp.where((solid_mask == 0) & inside[None], BLOCK_LIMIT, 0.0).astype(jnp.float32)
    adjoint = adjoint_in
    raw = jnp.zeros((width_x, width_y), jnp.float32)
    for section in (1, 0):
        pulled = pull_back(halo(adjoint, 1), width_x, width_y)
        adjoint, term = adjoint_step(section, pulled, forward_pops, blocking, lever)
        raw = raw + term
    raw = SENSE_SCALE * raw
    smooth = helmholtz(raw, SWEEPS)
    region_one = (region_label == 1).astype(jnp.float32)
    region_two = (region_label == 2).astype(jnp.float32)
    stats = jnp.stack(
        [
            jnp.sum(smooth * region_one),
            jnp.sum(smooth * region_two),
            jnp.sum(region_one),
            jnp.sum(region_two),
        ]
    )
    stats = lax.psum(stats, ("gx", "gy"))
    means = stats[:2] / jnp.maximum(stats[2:], 1.0)
    sensitivity = region_one * (smooth - means[0]) + region_two * (smooth - means[1])
    return (adjoint, sensitivity)


def solution(mesh):
    in_specs = (
        P(None, None, "gx", "gy"),
        P(None, None, None, "gx", "gy"),
        P(None, "gx", "gy"),
        P("gx", "gy"),
        P("gx", "gy"),
    )
    out_specs = (P(None, None, "gx", "gy"), P("gx", "gy"))
    return jax.shard_map(
        per_device, mesh=mesh, in_specs=in_specs, out_specs=out_specs, check_vma=False
    )
```

```python
import jax
import jax.numpy as jnp
from jax import lax
from jax.sharding import PartitionSpec as P

SWEEPS = 4


VELOCITIES = [
    (0, 0, 0),
    (1, 0, 0),
    (-1, 0, 0),
    (0, 1, 0),
    (0, -1, 0),
    (0, 0, 1),
    (0, 0, -1),
    (1, 1, 0),
    (-1, -1, 0),
    (1, -1, 0),
    (-1, 1, 0),
    (1, 0, 1),
    (-1, 0, -1),
    (1, 0, -1),
    (-1, 0, 1),
    (0, 1, 1),
    (0, -1, -1),
    (0, 1, -1),
    (0, -1, 1),
]
OPPOSITE = [0, 2, 1, 4, 3, 6, 5, 8, 7, 10, 9, 12, 11, 14, 13, 16, 15, 18, 17]
WEIGHTS = [1.0 / 3.0] + [1.0 / 18.0] * 6 + [1.0 / 36.0] * 12
RELAX_RATES = [0.0] * 4 + [1.6] * 6 + [1.4] * 6 + [1.2] * 3
EXPONENTS = [
    (0, 0, 0),
    (1, 0, 0),
    (0, 1, 0),
    (0, 0, 1),
    (2, 0, 0),
    (0, 2, 0),
    (0, 0, 2),
    (1, 1, 0),
    (1, 0, 1),
    (0, 1, 1),
    (2, 1, 0),
    (2, 0, 1),
    (1, 2, 0),
    (0, 2, 1),
    (1, 0, 2),
    (0, 1, 2),
    (2, 2, 0),
    (2, 0, 2),
    (0, 2, 2),
]
BLOCK_LIMIT = 0.5
SENSE_SCALE = 20.0
FILTER_WEIGHT = 16.0

import functools

from jax.experimental import pallas as pl
from jax.experimental.pallas import tpu as pltpu

def moment_table():
    rows_out = []
    for expo in EXPONENTS:
        vector = [
            float(vel[0] ** expo[0] * vel[1] ** expo[1] * vel[2] ** expo[2]) for vel in VELOCITIES
        ]
        for prior in rows_out:
            factor = sum((a * b for a, b in zip(vector, prior))) / sum((b * b for b in prior))
            vector = [a - factor * b for a, b in zip(vector, prior)]
        rows_out.append(vector)
    norms = [sum((b * b for b in row)) for row in rows_out]
    table = []
    for first in range(19):
        line = []
        for second in range(19):
            line.append(
                sum(
                    (
                        rows_out[k][first] / norms[k] * RELAX_RATES[k] * rows_out[k][second]
                        for k in range(19)
                    )
                )
            )
        table.append(line)
    return table


RELAX = moment_table()


def halo(cells, w):
    for axis, dim in (("gx", -2), ("gy", -1)):
        count = lax.axis_size(axis)
        size = cells.shape[dim]
        head = lax.slice_in_dim(cells, 0, w, axis=cells.ndim + dim)
        tail = lax.slice_in_dim(cells, size - w, size, axis=cells.ndim + dim)
        low = lax.ppermute(tail, axis, [(i, i + 1) for i in range(count - 1)])
        high = lax.ppermute(head, axis, [(i + 1, i) for i in range(count - 1)])
        cells = jnp.concatenate([low, cells, high], axis=dim)
    return cells


def global_sum(values):
    nx = lax.axis_size("gx")
    ny = lax.axis_size("gy")
    total = nx * ny
    bits = total.bit_length() - 1
    assert 1 << bits == total
    for k in range(bits):
        values = values + lax.ppermute(values, ("gx", "gy"), [(i, i ^ (1 << k)) for i in range(total)])
    return values


def pull_back(ext, width_x, width_y):
    pieces = []
    for slot in range(19):
        step_x, step_y, step_z = VELOCITIES[slot]
        piece = ext[slot, :, 1 + step_x : 1 + step_x + width_x, 1 + step_y : 1 + step_y + width_y]
        pieces.append(jnp.roll(piece, -step_z, axis=0))
    return jnp.stack(pieces)


def cell_math(g, f, b, lev):
    rho = f[0]
    for i in range(1, 19):
        rho = rho + f[i]
    mom = []
    for d in range(3):
        acc = None
        for i in range(19):
            c = VELOCITIES[i][d]
            if c == 0:
                continue
            acc = (f[i] if acc is None else acc + f[i]) if c > 0 else (-f[i] if acc is None else acc - f[i])
        mom.append(acc)
    u = [m / rho for m in mom]
    usq = u[0] * u[0] + u[1] * u[1] + u[2] * u[2]
    one_b = 1.0 - b
    q = []
    for j in range(19):
        acc = None
        for l in range(19):
            t = RELAX[j][l] * g[l]
            acc = t if acc is None else acc + t
        q.append(acc)
    tsum = None
    for i in range(19):
        cu = None
        for d in range(3):
            c = VELOCITIES[i][d]
            if c == 0:
                continue
            cu = (u[d] if c > 0 else -u[d]) if cu is None else (cu + u[d] if c > 0 else cu - u[d])
        if cu is None:
            phi = 1.0 - 1.5 * usq
        else:
            phi = 1.0 + 3.0 * cu + 4.5 * cu * cu - 1.5 * usq
        eq = WEIGHTS[i] * rho * phi
        t = g[i] * (f[OPPOSITE[i]] - f[i]) + q[i] * (f[i] - eq)
        tsum = t if tsum is None else tsum + t
    term = lev * tsum
    k = [one_b * qj for qj in q]
    wk = [WEIGHTS[i] * k[i] for i in range(19)]
    a_sum = wk[0]
    for i in range(1, 19):
        a_sum = a_sum + wk[i]
    bvec = []
    for d in range(3):
        acc = None
        for i in range(19):
            c = VELOCITIES[i][d]
            if c == 0:
                continue
            acc = (wk[i] if acc is None else acc + wk[i]) if c > 0 else (-wk[i] if acc is None else acc - wk[i])
        bvec.append(acc)
    cmat = {}
    for d in range(3):
        for e in range(d, 3):
            acc = None
            for i in range(19):
                c = VELOCITIES[i][d] * VELOCITIES[i][e]
                if c == 0:
                    continue
                acc = (wk[i] if acc is None else acc + wk[i]) if c > 0 else (-wk[i] if acc is None else acc - wk[i])
            cmat[(d, e)] = acc
            cmat[(e, d)] = acc
    cu_vec = [cmat[(d, 0)] * u[0] + cmat[(d, 1)] * u[1] + cmat[(d, 2)] * u[2] for d in range(3)]
    ucu = u[0] * cu_vec[0] + u[1] * cu_vec[1] + u[2] * cu_vec[2]
    e_val = a_sum - 4.5 * ucu + 1.5 * a_sum * usq
    gvec = [3.0 * bvec[d] + 9.0 * cu_vec[d] - 3.0 * a_sum * u[d] for d in range(3)]
    result = []
    for j in range(19):
        r = one_b * g[j] - k[j] + e_val + b * g[OPPOSITE[j]]
        for d in range(3):
            c = VELOCITIES[j][d]
            if c > 0:
                r = r + gvec[d]
            elif c < 0:
                r = r - gvec[d]
        result.append(r)
    return result, term


def step_kernel(section, rows, g_ref, f_ref, b_ref, l_ref, res_ref, term_ref):
    planes, width_x, _ = b_ref.shape
    chunks = width_x // rows

    def body(idx, acc):
        z = idx // chunks
        x0 = pl.multiple_of((idx % chunks) * rows, rows)
        xs = pl.ds(x0, rows)
        g = [g_ref[i, z, xs, :] for i in range(19)]
        f = [f_ref[section, i, z, xs, :].astype(jnp.float32) for i in range(19)]
        b = b_ref[z, xs, :]
        lev = l_ref[z, xs, :]
        result, term = cell_math(g, f, b, lev)
        for j in range(19):
            res_ref[j, z, xs, :] = result[j]
        term_ref[xs, :] = term_ref[xs, :] + term
        return acc

    term_ref[...] = jnp.zeros_like(term_ref)
    lax.fori_loop(0, planes * chunks, body, 0)


def adjoint_step(section, pulled, forward_pops, blocking, lever):
    _, planes, width_x, width_y = pulled.shape
    rows = 8 if width_x % 8 == 0 else width_x
    vmem = pl.BlockSpec(memory_space=pltpu.VMEM)
    return pl.pallas_call(
        functools.partial(step_kernel, section, rows),
        out_shape=(
            jax.ShapeDtypeStruct(pulled.shape, jnp.float32),
            jax.ShapeDtypeStruct((width_x, width_y), jnp.float32),
        ),
        in_specs=[vmem] * 4,
        out_specs=(vmem, vmem),
    )(pulled, forward_pops, blocking, lever)


def helmholtz(raw, w):
    scale_den = 1.0 + 4.0 * FILTER_WEIGHT
    width_x, width_y = raw.shape
    nx = lax.axis_size("gx")
    ny = lax.axis_size("gy")
    gxi = lax.axis_index("gx")
    gyi = lax.axis_index("gy")
    raw_ext = halo(raw, w)
    xs = gxi * width_x - w + lax.broadcasted_iota(jnp.int32, raw_ext.shape, 0)
    ys = gyi * width_y - w + lax.broadcasted_iota(jnp.int32, raw_ext.shape, 1)
    valid = (xs >= 0) & (xs < nx * width_x) & (ys >= 0) & (ys < ny * width_y)
    smooth = raw_ext
    for sweep in range(SWEEPS):
        framed = jnp.pad(smooth, 1)
        beside_all = framed[:-2, 1:-1] + framed[2:, 1:-1] + framed[1:-1, :-2] + framed[1:-1, 2:]
        smooth = jnp.where(valid, (raw_ext + FILTER_WEIGHT * beside_all) / scale_den, 0.0)
    return smooth[w:-w, w:-w]


def per_device(adjoint_in, forward_pops, solid_mask, region_label, design):
    planes, width_x, width_y = solid_mask.shape
    inside = region_label > 0
    blocking = jnp.where(
        solid_mask == 1, 1.0, jnp.where(inside[None], BLOCK_LIMIT * design[None], 0.0)
    ).astype(jnp.float32)
    lever = jnp.where((solid_mask == 0) & inside[None], BLOCK_LIMIT, 0.0).astype(jnp.float32)
    adjoint = adjoint_in
    raw = jnp.zeros((width_x, width_y), jnp.float32)
    for section in (1, 0):
        pulled = pull_back(halo(adjoint, 1), width_x, width_y)
        adjoint, term = adjoint_step(section, pulled, forward_pops, blocking, lever)
        raw = raw + term
    raw = SENSE_SCALE * raw
    smooth = helmholtz(raw, SWEEPS)
    region_one = (region_label == 1).astype(jnp.float32)
    region_two = (region_label == 2).astype(jnp.float32)
    stats = jnp.stack(
        [
            jnp.sum(smooth * region_one),
            jnp.sum(smooth * region_two),
            jnp.sum(region_one),
            jnp.sum(region_two),
        ]
    )
    stats = global_sum(stats)
    means = stats[:2] / jnp.maximum(stats[2:], 1.0)
    sensitivity = region_one * (smooth - means[0]) + region_two * (smooth - means[1])
    return (adjoint, sensitivity)


def solution(mesh):
    in_specs = (
        P(None, None, "gx", "gy"),
        P(None, None, None, "gx", "gy"),
        P(None, "gx", "gy"),
        P("gx", "gy"),
        P("gx", "gy"),
    )
    out_specs = (P(None, None, "gx", "gy"), P("gx", "gy"))
    return jax.shard_map(
        per_device, mesh=mesh, in_specs=in_specs, out_specs=out_specs, check_vma=False
    )
```

```python
import jax
import jax.numpy as jnp
from jax import lax
from jax.sharding import PartitionSpec as P

SWEEPS = 4


VELOCITIES = [
    (0, 0, 0),
    (1, 0, 0),
    (-1, 0, 0),
    (0, 1, 0),
    (0, -1, 0),
    (0, 0, 1),
    (0, 0, -1),
    (1, 1, 0),
    (-1, -1, 0),
    (1, -1, 0),
    (-1, 1, 0),
    (1, 0, 1),
    (-1, 0, -1),
    (1, 0, -1),
    (-1, 0, 1),
    (0, 1, 1),
    (0, -1, -1),
    (0, 1, -1),
    (0, -1, 1),
]
OPPOSITE = [0, 2, 1, 4, 3, 6, 5, 8, 7, 10, 9, 12, 11, 14, 13, 16, 15, 18, 17]
WEIGHTS = [1.0 / 3.0] + [1.0 / 18.0] * 6 + [1.0 / 36.0] * 12
RELAX_RATES = [0.0] * 4 + [1.6] * 6 + [1.4] * 6 + [1.2] * 3
EXPONENTS = [
    (0, 0, 0),
    (1, 0, 0),
    (0, 1, 0),
    (0, 0, 1),
    (2, 0, 0),
    (0, 2, 0),
    (0, 0, 2),
    (1, 1, 0),
    (1, 0, 1),
    (0, 1, 1),
    (2, 1, 0),
    (2, 0, 1),
    (1, 2, 0),
    (0, 2, 1),
    (1, 0, 2),
    (0, 1, 2),
    (2, 2, 0),
    (2, 0, 2),
    (0, 2, 2),
]
BLOCK_LIMIT = 0.5
SENSE_SCALE = 20.0
FILTER_WEIGHT = 16.0

import functools

from jax.experimental import pallas as pl
from jax.experimental.pallas import tpu as pltpu

def moment_table():
    rows_out = []
    for expo in EXPONENTS:
        vector = [
            float(vel[0] ** expo[0] * vel[1] ** expo[1] * vel[2] ** expo[2]) for vel in VELOCITIES
        ]
        for prior in rows_out:
            factor = sum((a * b for a, b in zip(vector, prior))) / sum((b * b for b in prior))
            vector = [a - factor * b for a, b in zip(vector, prior)]
        rows_out.append(vector)
    norms = [sum((b * b for b in row)) for row in rows_out]
    table = []
    for first in range(19):
        line = []
        for second in range(19):
            line.append(
                sum(
                    (
                        rows_out[k][first] / norms[k] * RELAX_RATES[k] * rows_out[k][second]
                        for k in range(19)
                    )
                )
            )
        table.append(line)
    return table


RELAX = moment_table()


def halo(cells, w):
    for axis, dim in (("gx", -2), ("gy", -1)):
        count = lax.axis_size(axis)
        size = cells.shape[dim]
        head = lax.slice_in_dim(cells, 0, w, axis=cells.ndim + dim)
        tail = lax.slice_in_dim(cells, size - w, size, axis=cells.ndim + dim)
        low = lax.ppermute(tail, axis, [(i, i + 1) for i in range(count - 1)])
        high = lax.ppermute(head, axis, [(i + 1, i) for i in range(count - 1)])
        cells = jnp.concatenate([low, cells, high], axis=dim)
    return cells


def global_sum(values):
    values = lax.psum(values, "gx")
    ny = lax.axis_size("gy")
    bits = ny.bit_length() - 1
    assert 1 << bits == ny
    for k in range(bits):
        values = values + lax.ppermute(values, "gy", [(i, i ^ (1 << k)) for i in range(ny)])
    return values


def pull_back(ext, width_x, width_y):
    pieces = []
    for slot in range(19):
        step_x, step_y, step_z = VELOCITIES[slot]
        piece = ext[slot, :, 1 + step_x : 1 + step_x + width_x, 1 + step_y : 1 + step_y + width_y]
        pieces.append(jnp.roll(piece, -step_z, axis=0))
    return jnp.stack(pieces)


def cell_math(g, f, b, lev):
    rho = f[0]
    for i in range(1, 19):
        rho = rho + f[i]
    mom = []
    for d in range(3):
        acc = None
        for i in range(19):
            c = VELOCITIES[i][d]
            if c == 0:
                continue
            acc = (f[i] if acc is None else acc + f[i]) if c > 0 else (-f[i] if acc is None else acc - f[i])
        mom.append(acc)
    u = [m / rho for m in mom]
    usq = u[0] * u[0] + u[1] * u[1] + u[2] * u[2]
    one_b = 1.0 - b
    q = []
    for j in range(19):
        acc = None
        for l in range(19):
            t = RELAX[j][l] * g[l]
            acc = t if acc is None else acc + t
        q.append(acc)
    tsum = None
    for i in range(19):
        cu = None
        for d in range(3):
            c = VELOCITIES[i][d]
            if c == 0:
                continue
            cu = (u[d] if c > 0 else -u[d]) if cu is None else (cu + u[d] if c > 0 else cu - u[d])
        if cu is None:
            phi = 1.0 - 1.5 * usq
        else:
            phi = 1.0 + 3.0 * cu + 4.5 * cu * cu - 1.5 * usq
        eq = WEIGHTS[i] * rho * phi
        t = g[i] * (f[OPPOSITE[i]] - f[i]) + q[i] * (f[i] - eq)
        tsum = t if tsum is None else tsum + t
    term = lev * tsum
    k = [one_b * qj for qj in q]
    wk = [WEIGHTS[i] * k[i] for i in range(19)]
    a_sum = wk[0]
    for i in range(1, 19):
        a_sum = a_sum + wk[i]
    bvec = []
    for d in range(3):
        acc = None
        for i in range(19):
            c = VELOCITIES[i][d]
            if c == 0:
                continue
            acc = (wk[i] if acc is None else acc + wk[i]) if c > 0 else (-wk[i] if acc is None else acc - wk[i])
        bvec.append(acc)
    cmat = {}
    for d in range(3):
        for e in range(d, 3):
            acc = None
            for i in range(19):
                c = VELOCITIES[i][d] * VELOCITIES[i][e]
                if c == 0:
                    continue
                acc = (wk[i] if acc is None else acc + wk[i]) if c > 0 else (-wk[i] if acc is None else acc - wk[i])
            cmat[(d, e)] = acc
            cmat[(e, d)] = acc
    cu_vec = [cmat[(d, 0)] * u[0] + cmat[(d, 1)] * u[1] + cmat[(d, 2)] * u[2] for d in range(3)]
    ucu = u[0] * cu_vec[0] + u[1] * cu_vec[1] + u[2] * cu_vec[2]
    e_val = a_sum - 4.5 * ucu + 1.5 * a_sum * usq
    gvec = [3.0 * bvec[d] + 9.0 * cu_vec[d] - 3.0 * a_sum * u[d] for d in range(3)]
    result = []
    for j in range(19):
        r = one_b * g[j] - k[j] + e_val + b * g[OPPOSITE[j]]
        for d in range(3):
            c = VELOCITIES[j][d]
            if c > 0:
                r = r + gvec[d]
            elif c < 0:
                r = r - gvec[d]
        result.append(r)
    return result, term


def step_kernel(section, rows, g_ref, f_ref, b_ref, l_ref, res_ref, term_ref):
    planes, width_x, _ = b_ref.shape
    chunks = width_x // rows

    def body(idx, acc):
        z = idx // chunks
        x0 = pl.multiple_of((idx % chunks) * rows, rows)
        xs = pl.ds(x0, rows)
        g = [g_ref[i, z, xs, :] for i in range(19)]
        f = [f_ref[section, i, z, xs, :].astype(jnp.float32) for i in range(19)]
        b = b_ref[z, xs, :]
        lev = l_ref[z, xs, :]
        result, term = cell_math(g, f, b, lev)
        for j in range(19):
            res_ref[j, z, xs, :] = result[j]
        term_ref[xs, :] = term_ref[xs, :] + term
        return acc

    term_ref[...] = jnp.zeros_like(term_ref)
    lax.fori_loop(0, planes * chunks, body, 0)


def adjoint_step(section, pulled, forward_pops, blocking, lever):
    _, planes, width_x, width_y = pulled.shape
    rows = 8 if width_x % 8 == 0 else width_x
    vmem = pl.BlockSpec(memory_space=pltpu.VMEM)
    return pl.pallas_call(
        functools.partial(step_kernel, section, rows),
        out_shape=(
            jax.ShapeDtypeStruct(pulled.shape, jnp.float32),
            jax.ShapeDtypeStruct((width_x, width_y), jnp.float32),
        ),
        in_specs=[vmem] * 4,
        out_specs=(vmem, vmem),
    )(pulled, forward_pops, blocking, lever)


def helmholtz(raw, w):
    scale_den = 1.0 + 4.0 * FILTER_WEIGHT
    width_x, width_y = raw.shape
    nx = lax.axis_size("gx")
    ny = lax.axis_size("gy")
    gxi = lax.axis_index("gx")
    gyi = lax.axis_index("gy")
    raw_ext = halo(raw, w)
    xs = gxi * width_x - w + lax.broadcasted_iota(jnp.int32, raw_ext.shape, 0)
    ys = gyi * width_y - w + lax.broadcasted_iota(jnp.int32, raw_ext.shape, 1)
    valid = (xs >= 0) & (xs < nx * width_x) & (ys >= 0) & (ys < ny * width_y)
    smooth = raw_ext
    for sweep in range(SWEEPS):
        framed = jnp.pad(smooth, 1)
        beside_all = framed[:-2, 1:-1] + framed[2:, 1:-1] + framed[1:-1, :-2] + framed[1:-1, 2:]
        smooth = jnp.where(valid, (raw_ext + FILTER_WEIGHT * beside_all) / scale_den, 0.0)
    return smooth[w:-w, w:-w]


def per_device(adjoint_in, forward_pops, solid_mask, region_label, design):
    planes, width_x, width_y = solid_mask.shape
    inside = region_label > 0
    blocking = jnp.where(
        solid_mask == 1, 1.0, jnp.where(inside[None], BLOCK_LIMIT * design[None], 0.0)
    ).astype(jnp.float32)
    lever = jnp.where((solid_mask == 0) & inside[None], BLOCK_LIMIT, 0.0).astype(jnp.float32)
    adjoint = adjoint_in
    raw = jnp.zeros((width_x, width_y), jnp.float32)
    for section in (1, 0):
        pulled = pull_back(halo(adjoint, 1), width_x, width_y)
        adjoint, term = adjoint_step(section, pulled, forward_pops, blocking, lever)
        raw = raw + term
    raw = SENSE_SCALE * raw
    smooth = helmholtz(raw, SWEEPS)
    region_one = (region_label == 1).astype(jnp.float32)
    region_two = (region_label == 2).astype(jnp.float32)
    stats = jnp.stack(
        [
            jnp.sum(smooth * region_one),
            jnp.sum(smooth * region_two),
            jnp.sum(region_one),
            jnp.sum(region_two),
        ]
    )
    stats = global_sum(stats)
    means = stats[:2] / jnp.maximum(stats[2:], 1.0)
    sensitivity = region_one * (smooth - means[0]) + region_two * (smooth - means[1])
    return (adjoint, sensitivity)


def solution(mesh):
    in_specs = (
        P(None, None, "gx", "gy"),
        P(None, None, None, "gx", "gy"),
        P(None, "gx", "gy"),
        P("gx", "gy"),
        P("gx", "gy"),
    )
    out_specs = (P(None, None, "gx", "gy"), P("gx", "gy"))
    return jax.shard_map(
        per_device, mesh=mesh, in_specs=in_specs, out_specs=out_specs, check_vma=False
    )
```

```python
import jax
import jax.numpy as jnp
from jax import lax
from jax.sharding import PartitionSpec as P

SWEEPS = 4


VELOCITIES = [
    (0, 0, 0),
    (1, 0, 0),
    (-1, 0, 0),
    (0, 1, 0),
    (0, -1, 0),
    (0, 0, 1),
    (0, 0, -1),
    (1, 1, 0),
    (-1, -1, 0),
    (1, -1, 0),
    (-1, 1, 0),
    (1, 0, 1),
    (-1, 0, -1),
    (1, 0, -1),
    (-1, 0, 1),
    (0, 1, 1),
    (0, -1, -1),
    (0, 1, -1),
    (0, -1, 1),
]
OPPOSITE = [0, 2, 1, 4, 3, 6, 5, 8, 7, 10, 9, 12, 11, 14, 13, 16, 15, 18, 17]
WEIGHTS = [1.0 / 3.0] + [1.0 / 18.0] * 6 + [1.0 / 36.0] * 12
RELAX_RATES = [0.0] * 4 + [1.6] * 6 + [1.4] * 6 + [1.2] * 3
EXPONENTS = [
    (0, 0, 0),
    (1, 0, 0),
    (0, 1, 0),
    (0, 0, 1),
    (2, 0, 0),
    (0, 2, 0),
    (0, 0, 2),
    (1, 1, 0),
    (1, 0, 1),
    (0, 1, 1),
    (2, 1, 0),
    (2, 0, 1),
    (1, 2, 0),
    (0, 2, 1),
    (1, 0, 2),
    (0, 1, 2),
    (2, 2, 0),
    (2, 0, 2),
    (0, 2, 2),
]
BLOCK_LIMIT = 0.5
SENSE_SCALE = 20.0
FILTER_WEIGHT = 16.0

import functools

from jax.experimental import pallas as pl
from jax.experimental.pallas import tpu as pltpu

def moment_table():
    rows_out = []
    for expo in EXPONENTS:
        vector = [
            float(vel[0] ** expo[0] * vel[1] ** expo[1] * vel[2] ** expo[2]) for vel in VELOCITIES
        ]
        for prior in rows_out:
            factor = sum((a * b for a, b in zip(vector, prior))) / sum((b * b for b in prior))
            vector = [a - factor * b for a, b in zip(vector, prior)]
        rows_out.append(vector)
    norms = [sum((b * b for b in row)) for row in rows_out]
    table = []
    for first in range(19):
        line = []
        for second in range(19):
            line.append(
                sum(
                    (
                        rows_out[k][first] / norms[k] * RELAX_RATES[k] * rows_out[k][second]
                        for k in range(19)
                    )
                )
            )
        table.append(line)
    return table


RELAX = moment_table()


def halo(cells, w):
    for axis, dim in (("gx", -2), ("gy", -1)):
        count = lax.axis_size(axis)
        size = cells.shape[dim]
        head = lax.slice_in_dim(cells, 0, w, axis=cells.ndim + dim)
        tail = lax.slice_in_dim(cells, size - w, size, axis=cells.ndim + dim)
        low = lax.ppermute(tail, axis, [(i, i + 1) for i in range(count - 1)])
        high = lax.ppermute(head, axis, [(i + 1, i) for i in range(count - 1)])
        cells = jnp.concatenate([low, cells, high], axis=dim)
    return cells


def global_sum(values):
    values = lax.psum(values, "gx")
    ny = lax.axis_size("gy")
    bits = ny.bit_length() - 1
    assert 1 << bits == ny
    for k in range(bits):
        values = values + lax.ppermute(values, "gy", [(i, i ^ (1 << k)) for i in range(ny)])
    return values


def pull_back(ext, width_x, width_y):
    pieces = []
    for slot in range(19):
        step_x, step_y, step_z = VELOCITIES[slot]
        piece = ext[slot, :, 1 + step_x : 1 + step_x + width_x, 1 + step_y : 1 + step_y + width_y]
        pieces.append(jnp.roll(piece, -step_z, axis=0))
    return jnp.stack(pieces)


def cell_math(g, f, b, lev):
    rho = f[0]
    for i in range(1, 19):
        rho = rho + f[i]
    mom = []
    for d in range(3):
        acc = None
        for i in range(19):
            c = VELOCITIES[i][d]
            if c == 0:
                continue
            acc = (f[i] if acc is None else acc + f[i]) if c > 0 else (-f[i] if acc is None else acc - f[i])
        mom.append(acc)
    u = [m / rho for m in mom]
    usq = u[0] * u[0] + u[1] * u[1] + u[2] * u[2]
    one_b = 1.0 - b
    q = []
    for j in range(19):
        acc = None
        for l in range(19):
            t = RELAX[j][l] * g[l]
            acc = t if acc is None else acc + t
        q.append(acc)
    tsum = None
    for i in range(19):
        cu = None
        for d in range(3):
            c = VELOCITIES[i][d]
            if c == 0:
                continue
            cu = (u[d] if c > 0 else -u[d]) if cu is None else (cu + u[d] if c > 0 else cu - u[d])
        if cu is None:
            phi = 1.0 - 1.5 * usq
        else:
            phi = 1.0 + 3.0 * cu + 4.5 * cu * cu - 1.5 * usq
        eq = WEIGHTS[i] * rho * phi
        t = g[i] * (f[OPPOSITE[i]] - f[i]) + q[i] * (f[i] - eq)
        tsum = t if tsum is None else tsum + t
    term = lev * tsum
    k = [one_b * qj for qj in q]
    wk = [WEIGHTS[i] * k[i] for i in range(19)]
    a_sum = wk[0]
    for i in range(1, 19):
        a_sum = a_sum + wk[i]
    bvec = []
    for d in range(3):
        acc = None
        for i in range(19):
            c = VELOCITIES[i][d]
            if c == 0:
                continue
            acc = (wk[i] if acc is None else acc + wk[i]) if c > 0 else (-wk[i] if acc is None else acc - wk[i])
        bvec.append(acc)
    cmat = {}
    for d in range(3):
        for e in range(d, 3):
            acc = None
            for i in range(19):
                c = VELOCITIES[i][d] * VELOCITIES[i][e]
                if c == 0:
                    continue
                acc = (wk[i] if acc is None else acc + wk[i]) if c > 0 else (-wk[i] if acc is None else acc - wk[i])
            cmat[(d, e)] = acc
            cmat[(e, d)] = acc
    cu_vec = [cmat[(d, 0)] * u[0] + cmat[(d, 1)] * u[1] + cmat[(d, 2)] * u[2] for d in range(3)]
    ucu = u[0] * cu_vec[0] + u[1] * cu_vec[1] + u[2] * cu_vec[2]
    e_val = a_sum - 4.5 * ucu + 1.5 * a_sum * usq
    gvec = [3.0 * bvec[d] + 9.0 * cu_vec[d] - 3.0 * a_sum * u[d] for d in range(3)]
    result = []
    for j in range(19):
        r = one_b * g[j] - k[j] + e_val + b * g[OPPOSITE[j]]
        for d in range(3):
            c = VELOCITIES[j][d]
            if c > 0:
                r = r + gvec[d]
            elif c < 0:
                r = r - gvec[d]
        result.append(r)
    return result, term


def step_kernel(section, rows, a_ref, f_ref, b_ref, l_ref, res_ref, term_ref):
    planes, width_x, width_y = b_ref.shape
    chunks = width_x // rows

    def body(z, acc):
        for chunk in range(chunks):
            x0 = chunk * rows
            xs = pl.ds(x0, rows)
            g = []
            for i in range(19):
                step_x, step_y, step_z = VELOCITIES[i]
                zz = (z + step_z + planes) % planes
                g.append(a_ref[i, zz, pl.ds(x0 + 1 + step_x, rows), pl.ds(1 + step_y, width_y)])
            f = [f_ref[section, i, z, xs, :].astype(jnp.float32) for i in range(19)]
            b = b_ref[z, xs, :]
            lev = l_ref[z, xs, :]
            result, term = cell_math(g, f, b, lev)
            for j in range(19):
                res_ref[j, z, xs, :] = result[j]
            term_ref[xs, :] = term_ref[xs, :] + term
        return acc

    term_ref[...] = jnp.zeros_like(term_ref)
    lax.fori_loop(0, planes, body, 0)


def adjoint_step(section, ext, forward_pops, blocking, lever):
    planes, width_x, width_y = blocking.shape
    rows = 8 if width_x % 8 == 0 else width_x
    vmem = pl.BlockSpec(memory_space=pltpu.VMEM)
    return pl.pallas_call(
        functools.partial(step_kernel, section, rows),
        out_shape=(
            jax.ShapeDtypeStruct((19, planes, width_x, width_y), jnp.float32),
            jax.ShapeDtypeStruct((width_x, width_y), jnp.float32),
        ),
        in_specs=[vmem] * 4,
        out_specs=(vmem, vmem),
    )(ext, forward_pops, blocking, lever)


def helmholtz(raw, w):
    scale_den = 1.0 + 4.0 * FILTER_WEIGHT
    width_x, width_y = raw.shape
    nx = lax.axis_size("gx")
    ny = lax.axis_size("gy")
    gxi = lax.axis_index("gx")
    gyi = lax.axis_index("gy")
    raw_ext = halo(raw, w)
    xs = gxi * width_x - w + lax.broadcasted_iota(jnp.int32, raw_ext.shape, 0)
    ys = gyi * width_y - w + lax.broadcasted_iota(jnp.int32, raw_ext.shape, 1)
    valid = (xs >= 0) & (xs < nx * width_x) & (ys >= 0) & (ys < ny * width_y)
    smooth = raw_ext
    for sweep in range(SWEEPS):
        framed = jnp.pad(smooth, 1)
        beside_all = framed[:-2, 1:-1] + framed[2:, 1:-1] + framed[1:-1, :-2] + framed[1:-1, 2:]
        smooth = jnp.where(valid, (raw_ext + FILTER_WEIGHT * beside_all) / scale_den, 0.0)
    return smooth[w:-w, w:-w]


def per_device(adjoint_in, forward_pops, solid_mask, region_label, design):
    planes, width_x, width_y = solid_mask.shape
    inside = region_label > 0
    blocking = jnp.where(
        solid_mask == 1, 1.0, jnp.where(inside[None], BLOCK_LIMIT * design[None], 0.0)
    ).astype(jnp.float32)
    lever = jnp.where((solid_mask == 0) & inside[None], BLOCK_LIMIT, 0.0).astype(jnp.float32)
    adjoint = adjoint_in
    raw = jnp.zeros((width_x, width_y), jnp.float32)
    for section in (1, 0):
        adjoint, term = adjoint_step(section, halo(adjoint, 1), forward_pops, blocking, lever)
        raw = raw + term
    raw = SENSE_SCALE * raw
    smooth = helmholtz(raw, SWEEPS)
    region_one = (region_label == 1).astype(jnp.float32)
    region_two = (region_label == 2).astype(jnp.float32)
    stats = jnp.stack(
        [
            jnp.sum(smooth * region_one),
            jnp.sum(smooth * region_two),
            jnp.sum(region_one),
            jnp.sum(region_two),
        ]
    )
    stats = global_sum(stats)
    means = stats[:2] / jnp.maximum(stats[2:], 1.0)
    sensitivity = region_one * (smooth - means[0]) + region_two * (smooth - means[1])
    return (adjoint, sensitivity)


def solution(mesh):
    in_specs = (
        P(None, None, "gx", "gy"),
        P(None, None, None, "gx", "gy"),
        P(None, "gx", "gy"),
        P("gx", "gy"),
        P("gx", "gy"),
    )
    out_specs = (P(None, None, "gx", "gy"), P("gx", "gy"))
    return jax.shard_map(
        per_device, mesh=mesh, in_specs=in_specs, out_specs=out_specs, check_vma=False
    )
```

```python
import jax
import jax.numpy as jnp
from jax import lax
from jax.sharding import PartitionSpec as P

SWEEPS = 4


VELOCITIES = [
    (0, 0, 0),
    (1, 0, 0),
    (-1, 0, 0),
    (0, 1, 0),
    (0, -1, 0),
    (0, 0, 1),
    (0, 0, -1),
    (1, 1, 0),
    (-1, -1, 0),
    (1, -1, 0),
    (-1, 1, 0),
    (1, 0, 1),
    (-1, 0, -1),
    (1, 0, -1),
    (-1, 0, 1),
    (0, 1, 1),
    (0, -1, -1),
    (0, 1, -1),
    (0, -1, 1),
]
OPPOSITE = [0, 2, 1, 4, 3, 6, 5, 8, 7, 10, 9, 12, 11, 14, 13, 16, 15, 18, 17]
WEIGHTS = [1.0 / 3.0] + [1.0 / 18.0] * 6 + [1.0 / 36.0] * 12
RELAX_RATES = [0.0] * 4 + [1.6] * 6 + [1.4] * 6 + [1.2] * 3
EXPONENTS = [
    (0, 0, 0),
    (1, 0, 0),
    (0, 1, 0),
    (0, 0, 1),
    (2, 0, 0),
    (0, 2, 0),
    (0, 0, 2),
    (1, 1, 0),
    (1, 0, 1),
    (0, 1, 1),
    (2, 1, 0),
    (2, 0, 1),
    (1, 2, 0),
    (0, 2, 1),
    (1, 0, 2),
    (0, 1, 2),
    (2, 2, 0),
    (2, 0, 2),
    (0, 2, 2),
]
BLOCK_LIMIT = 0.5
SENSE_SCALE = 20.0
FILTER_WEIGHT = 16.0

import functools

from jax.experimental import pallas as pl
from jax.experimental.pallas import tpu as pltpu

def moment_table():
    rows_out = []
    for expo in EXPONENTS:
        vector = [
            float(vel[0] ** expo[0] * vel[1] ** expo[1] * vel[2] ** expo[2]) for vel in VELOCITIES
        ]
        for prior in rows_out:
            factor = sum((a * b for a, b in zip(vector, prior))) / sum((b * b for b in prior))
            vector = [a - factor * b for a, b in zip(vector, prior)]
        rows_out.append(vector)
    norms = [sum((b * b for b in row)) for row in rows_out]
    table = []
    for first in range(19):
        line = []
        for second in range(19):
            line.append(
                sum(
                    (
                        rows_out[k][first] / norms[k] * RELAX_RATES[k] * rows_out[k][second]
                        for k in range(19)
                    )
                )
            )
        table.append(line)
    return table


RELAX = moment_table()


def halo(cells, w):
    return halo_many([cells], [w])[0]


def halo_many(arrays, widths):
    for axis, dim in (("gx", -2), ("gy", -1)):
        count = lax.axis_size(axis)
        heads, tails = [], []
        for a, w in zip(arrays, widths):
            size = a.shape[dim]
            heads.append(lax.slice_in_dim(a, 0, w, axis=a.ndim + dim))
            tails.append(lax.slice_in_dim(a, size - w, size, axis=a.ndim + dim))

        def send(pieces, pairs):
            if len(pieces) == 1:
                return [lax.ppermute(pieces[0], axis, pairs)]
            flat = jnp.concatenate([p.reshape(-1) for p in pieces])
            got = lax.ppermute(flat, axis, pairs)
            out, at = [], 0
            for p in pieces:
                out.append(got[at : at + p.size].reshape(p.shape))
                at += p.size
            return out

        lows = send(tails, [(i, i + 1) for i in range(count - 1)])
        highs = send(heads, [(i + 1, i) for i in range(count - 1)])
        arrays = [jnp.concatenate([lo, a, hi], axis=dim) for lo, a, hi in zip(lows, arrays, highs)]
    return arrays


def global_sum(values):
    values = lax.psum(values, "gx")
    ny = lax.axis_size("gy")
    bits = ny.bit_length() - 1
    assert 1 << bits == ny
    for k in range(bits):
        values = values + lax.ppermute(values, "gy", [(i, i ^ (1 << k)) for i in range(ny)])
    return values


def pull_back(ext, width_x, width_y):
    pieces = []
    for slot in range(19):
        step_x, step_y, step_z = VELOCITIES[slot]
        piece = ext[slot, :, 1 + step_x : 1 + step_x + width_x, 1 + step_y : 1 + step_y + width_y]
        pieces.append(jnp.roll(piece, -step_z, axis=0))
    return jnp.stack(pieces)


def cell_math(g, f, b, lev):
    rho = f[0]
    for i in range(1, 19):
        rho = rho + f[i]
    mom = []
    for d in range(3):
        acc = None
        for i in range(19):
            c = VELOCITIES[i][d]
            if c == 0:
                continue
            acc = (f[i] if acc is None else acc + f[i]) if c > 0 else (-f[i] if acc is None else acc - f[i])
        mom.append(acc)
    u = [m / rho for m in mom]
    usq = u[0] * u[0] + u[1] * u[1] + u[2] * u[2]
    one_b = 1.0 - b
    q = []
    for j in range(19):
        acc = None
        for l in range(19):
            t = RELAX[j][l] * g[l]
            acc = t if acc is None else acc + t
        q.append(acc)
    tsum = None
    for i in range(19):
        cu = None
        for d in range(3):
            c = VELOCITIES[i][d]
            if c == 0:
                continue
            cu = (u[d] if c > 0 else -u[d]) if cu is None else (cu + u[d] if c > 0 else cu - u[d])
        if cu is None:
            phi = 1.0 - 1.5 * usq
        else:
            phi = 1.0 + 3.0 * cu + 4.5 * cu * cu - 1.5 * usq
        eq = WEIGHTS[i] * rho * phi
        t = g[i] * (f[OPPOSITE[i]] - f[i]) + q[i] * (f[i] - eq)
        tsum = t if tsum is None else tsum + t
    term = lev * tsum
    k = [one_b * qj for qj in q]
    wk = [WEIGHTS[i] * k[i] for i in range(19)]
    a_sum = wk[0]
    for i in range(1, 19):
        a_sum = a_sum + wk[i]
    bvec = []
    for d in range(3):
        acc = None
        for i in range(19):
            c = VELOCITIES[i][d]
            if c == 0:
                continue
            acc = (wk[i] if acc is None else acc + wk[i]) if c > 0 else (-wk[i] if acc is None else acc - wk[i])
        bvec.append(acc)
    cmat = {}
    for d in range(3):
        for e in range(d, 3):
            acc = None
            for i in range(19):
                c = VELOCITIES[i][d] * VELOCITIES[i][e]
                if c == 0:
                    continue
                acc = (wk[i] if acc is None else acc + wk[i]) if c > 0 else (-wk[i] if acc is None else acc - wk[i])
            cmat[(d, e)] = acc
            cmat[(e, d)] = acc
    cu_vec = [cmat[(d, 0)] * u[0] + cmat[(d, 1)] * u[1] + cmat[(d, 2)] * u[2] for d in range(3)]
    ucu = u[0] * cu_vec[0] + u[1] * cu_vec[1] + u[2] * cu_vec[2]
    e_val = a_sum - 4.5 * ucu + 1.5 * a_sum * usq
    gvec = [3.0 * bvec[d] + 9.0 * cu_vec[d] - 3.0 * a_sum * u[d] for d in range(3)]
    result = []
    for j in range(19):
        r = one_b * g[j] - k[j] + e_val + b * g[OPPOSITE[j]]
        for d in range(3):
            c = VELOCITIES[j][d]
            if c > 0:
                r = r + gvec[d]
            elif c < 0:
                r = r - gvec[d]
        result.append(r)
    return result, term


def step_kernel(section, rows, g_ref, f_ref, b_ref, l_ref, res_ref, term_ref):
    planes, width_x, _ = b_ref.shape
    chunks = width_x // rows

    def body(idx, acc):
        z = idx // chunks
        x0 = pl.multiple_of((idx % chunks) * rows, rows)
        xs = pl.ds(x0, rows)
        g = [g_ref[i, z, xs, :] for i in range(19)]
        f = [f_ref[section, i, z, xs, :].astype(jnp.float32) for i in range(19)]
        b = b_ref[z, xs, :]
        lev = l_ref[z, xs, :]
        result, term = cell_math(g, f, b, lev)
        for j in range(19):
            res_ref[j, z, xs, :] = result[j]
        term_ref[xs, :] = term_ref[xs, :] + term
        return acc

    term_ref[...] = jnp.zeros_like(term_ref)
    lax.fori_loop(0, planes * chunks, body, 0)


def adjoint_step(section, pulled, forward_pops, blocking, lever):
    planes, width_x, width_y = blocking.shape
    rows = 8 if width_x % 8 == 0 else width_x
    vmem = pl.BlockSpec(memory_space=pltpu.VMEM)
    return pl.pallas_call(
        functools.partial(step_kernel, section, rows),
        out_shape=(
            jax.ShapeDtypeStruct((19, planes, width_x, width_y), jnp.float32),
            jax.ShapeDtypeStruct((width_x, width_y), jnp.float32),
        ),
        in_specs=[vmem] * 4,
        out_specs=(vmem, vmem),
    )(pulled, forward_pops, blocking, lever)


def helmholtz(raw, w):
    scale_den = 1.0 + 4.0 * FILTER_WEIGHT
    width_x, width_y = raw.shape
    nx = lax.axis_size("gx")
    ny = lax.axis_size("gy")
    gxi = lax.axis_index("gx")
    gyi = lax.axis_index("gy")
    raw_ext = halo(raw, w)
    xs = gxi * width_x - w + lax.broadcasted_iota(jnp.int32, raw_ext.shape, 0)
    ys = gyi * width_y - w + lax.broadcasted_iota(jnp.int32, raw_ext.shape, 1)
    valid = (xs >= 0) & (xs < nx * width_x) & (ys >= 0) & (ys < ny * width_y)
    smooth = raw_ext
    for sweep in range(SWEEPS):
        framed = jnp.pad(smooth, 1)
        beside_all = framed[:-2, 1:-1] + framed[2:, 1:-1] + framed[1:-1, :-2] + framed[1:-1, 2:]
        smooth = jnp.where(valid, (raw_ext + FILTER_WEIGHT * beside_all) / scale_den, 0.0)
    return smooth[w:-w, w:-w]


def pad_to(a, rows, cols):
    pad = [(0, 0)] * (a.ndim - 2) + [(0, rows - a.shape[-2]), (0, cols - a.shape[-1])]
    return jnp.pad(a, pad)


def per_device(adjoint_in, forward_pops, solid_mask, region_label, design):
    planes, width_x, width_y = solid_mask.shape
    inside = region_label > 0
    blocking = jnp.where(
        solid_mask == 1, 1.0, jnp.where(inside[None], BLOCK_LIMIT * design[None], 0.0)
    ).astype(jnp.float32)
    lever = jnp.where((solid_mask == 0) & inside[None], BLOCK_LIMIT, 0.0).astype(jnp.float32)
    saved_one = forward_pops[1].astype(jnp.float32)
    adj_ext, saved_ext, block_ext = halo_many([adjoint_in, saved_one, blocking], [2, 1, 1])
    ext_x, ext_y = width_x + 2, width_y + 2
    rows = -(-ext_x // 8) * 8
    cols = -(-ext_y // 128) * 128
    pulled = pad_to(pull_back(adj_ext, ext_x, ext_y), rows, cols)
    first, term_ext = adjoint_step(
        0,
        pulled,
        pad_to(saved_ext, rows, cols)[None],
        pad_to(block_ext, rows, cols),
        pad_to(jnp.pad(lever, ((0, 0), (1, 1), (1, 1))), rows, cols),
    )
    gxi = lax.axis_index("gx")
    gyi = lax.axis_index("gy")
    nx = lax.axis_size("gx")
    ny = lax.axis_size("gy")
    xs = gxi * width_x - 1 + lax.broadcasted_iota(jnp.int32, (ext_x, ext_y), 0)
    ys = gyi * width_y - 1 + lax.broadcasted_iota(jnp.int32, (ext_x, ext_y), 1)
    in_grid = (xs >= 0) & (xs < nx * width_x) & (ys >= 0) & (ys < ny * width_y)
    first = jnp.where(in_grid, first[:, :, :ext_x, :ext_y], 0.0)
    term_one = term_ext[1 : 1 + width_x, 1 : 1 + width_y]
    pulled = pull_back(first, width_x, width_y)
    adjoint, term_two = adjoint_step(0, pulled, forward_pops, blocking, lever)
    raw = SENSE_SCALE * (term_one + term_two)
    smooth = helmholtz(raw, SWEEPS)
    region_one = (region_label == 1).astype(jnp.float32)
    region_two = (region_label == 2).astype(jnp.float32)
    stats = jnp.stack(
        [
            jnp.sum(smooth * region_one),
            jnp.sum(smooth * region_two),
            jnp.sum(region_one),
            jnp.sum(region_two),
        ]
    )
    stats = global_sum(stats)
    means = stats[:2] / jnp.maximum(stats[2:], 1.0)
    sensitivity = region_one * (smooth - means[0]) + region_two * (smooth - means[1])
    return (adjoint, sensitivity)


def solution(mesh):
    in_specs = (
        P(None, None, "gx", "gy"),
        P(None, None, None, "gx", "gy"),
        P(None, "gx", "gy"),
        P("gx", "gy"),
        P("gx", "gy"),
    )
    out_specs = (P(None, None, "gx", "gy"), P("gx", "gy"))
    return jax.shard_map(
        per_device, mesh=mesh, in_specs=in_specs, out_specs=out_specs, check_vma=False
    )
```

```python
import jax
import jax.numpy as jnp
from jax import lax
from jax.sharding import PartitionSpec as P

SWEEPS = 4


VELOCITIES = [
    (0, 0, 0),
    (1, 0, 0),
    (-1, 0, 0),
    (0, 1, 0),
    (0, -1, 0),
    (0, 0, 1),
    (0, 0, -1),
    (1, 1, 0),
    (-1, -1, 0),
    (1, -1, 0),
    (-1, 1, 0),
    (1, 0, 1),
    (-1, 0, -1),
    (1, 0, -1),
    (-1, 0, 1),
    (0, 1, 1),
    (0, -1, -1),
    (0, 1, -1),
    (0, -1, 1),
]
OPPOSITE = [0, 2, 1, 4, 3, 6, 5, 8, 7, 10, 9, 12, 11, 14, 13, 16, 15, 18, 17]
WEIGHTS = [1.0 / 3.0] + [1.0 / 18.0] * 6 + [1.0 / 36.0] * 12
RELAX_RATES = [0.0] * 4 + [1.6] * 6 + [1.4] * 6 + [1.2] * 3
EXPONENTS = [
    (0, 0, 0),
    (1, 0, 0),
    (0, 1, 0),
    (0, 0, 1),
    (2, 0, 0),
    (0, 2, 0),
    (0, 0, 2),
    (1, 1, 0),
    (1, 0, 1),
    (0, 1, 1),
    (2, 1, 0),
    (2, 0, 1),
    (1, 2, 0),
    (0, 2, 1),
    (1, 0, 2),
    (0, 1, 2),
    (2, 2, 0),
    (2, 0, 2),
    (0, 2, 2),
]
BLOCK_LIMIT = 0.5
SENSE_SCALE = 20.0
FILTER_WEIGHT = 16.0

import functools

from jax.experimental import pallas as pl
from jax.experimental.pallas import tpu as pltpu

def moment_table():
    rows_out = []
    for expo in EXPONENTS:
        vector = [
            float(vel[0] ** expo[0] * vel[1] ** expo[1] * vel[2] ** expo[2]) for vel in VELOCITIES
        ]
        for prior in rows_out:
            factor = sum((a * b for a, b in zip(vector, prior))) / sum((b * b for b in prior))
            vector = [a - factor * b for a, b in zip(vector, prior)]
        rows_out.append(vector)
    norms = [sum((b * b for b in row)) for row in rows_out]
    table = []
    for first in range(19):
        line = []
        for second in range(19):
            line.append(
                sum(
                    (
                        rows_out[k][first] / norms[k] * RELAX_RATES[k] * rows_out[k][second]
                        for k in range(19)
                    )
                )
            )
        table.append(line)
    return table


RELAX = moment_table()


def halo(cells, w):
    return halo_many([cells], [w])[0]


def halo_many(arrays, widths):
    for axis, dim in (("gx", -2), ("gy", -1)):
        count = lax.axis_size(axis)
        heads, tails = [], []
        for a, w in zip(arrays, widths):
            size = a.shape[dim]
            heads.append(lax.slice_in_dim(a, 0, w, axis=a.ndim + dim))
            tails.append(lax.slice_in_dim(a, size - w, size, axis=a.ndim + dim))

        def send(pieces, pairs):
            if len(pieces) == 1:
                return [lax.ppermute(pieces[0], axis, pairs)]
            flat = jnp.concatenate([p.reshape(-1) for p in pieces])
            got = lax.ppermute(flat, axis, pairs)
            out, at = [], 0
            for p in pieces:
                out.append(got[at : at + p.size].reshape(p.shape))
                at += p.size
            return out

        lows = send(tails, [(i, i + 1) for i in range(count - 1)])
        highs = send(heads, [(i + 1, i) for i in range(count - 1)])
        arrays = [jnp.concatenate([lo, a, hi], axis=dim) for lo, a, hi in zip(lows, arrays, highs)]
    return arrays


def global_sum(values):
    values = lax.psum(values, "gx")
    ny = lax.axis_size("gy")
    bits = ny.bit_length() - 1
    assert 1 << bits == ny
    for k in range(bits):
        values = values + lax.ppermute(values, "gy", [(i, i ^ (1 << k)) for i in range(ny)])
    return values


def pull_back(ext, width_x, width_y):
    pieces = []
    for slot in range(19):
        step_x, step_y, step_z = VELOCITIES[slot]
        piece = ext[slot, :, 1 + step_x : 1 + step_x + width_x, 1 + step_y : 1 + step_y + width_y]
        pieces.append(jnp.roll(piece, -step_z, axis=0))
    return jnp.stack(pieces)


def cell_math(g, f, b, lev):
    rho = f[0]
    for i in range(1, 19):
        rho = rho + f[i]
    mom = []
    for d in range(3):
        acc = None
        for i in range(19):
            c = VELOCITIES[i][d]
            if c == 0:
                continue
            acc = (f[i] if acc is None else acc + f[i]) if c > 0 else (-f[i] if acc is None else acc - f[i])
        mom.append(acc)
    u = [m / rho for m in mom]
    usq = u[0] * u[0] + u[1] * u[1] + u[2] * u[2]
    one_b = 1.0 - b
    q = []
    for j in range(19):
        acc = None
        for l in range(19):
            t = RELAX[j][l] * g[l]
            acc = t if acc is None else acc + t
        q.append(acc)
    tsum = None
    for i in range(19):
        cu = None
        for d in range(3):
            c = VELOCITIES[i][d]
            if c == 0:
                continue
            cu = (u[d] if c > 0 else -u[d]) if cu is None else (cu + u[d] if c > 0 else cu - u[d])
        if cu is None:
            phi = 1.0 - 1.5 * usq
        else:
            phi = 1.0 + 3.0 * cu + 4.5 * cu * cu - 1.5 * usq
        eq = WEIGHTS[i] * rho * phi
        t = g[i] * (f[OPPOSITE[i]] - f[i]) + q[i] * (f[i] - eq)
        tsum = t if tsum is None else tsum + t
    term = lev * tsum
    k = [one_b * qj for qj in q]
    wk = [WEIGHTS[i] * k[i] for i in range(19)]
    a_sum = wk[0]
    for i in range(1, 19):
        a_sum = a_sum + wk[i]
    bvec = []
    for d in range(3):
        acc = None
        for i in range(19):
            c = VELOCITIES[i][d]
            if c == 0:
                continue
            acc = (wk[i] if acc is None else acc + wk[i]) if c > 0 else (-wk[i] if acc is None else acc - wk[i])
        bvec.append(acc)
    cmat = {}
    for d in range(3):
        for e in range(d, 3):
            acc = None
            for i in range(19):
                c = VELOCITIES[i][d] * VELOCITIES[i][e]
                if c == 0:
                    continue
                acc = (wk[i] if acc is None else acc + wk[i]) if c > 0 else (-wk[i] if acc is None else acc - wk[i])
            cmat[(d, e)] = acc
            cmat[(e, d)] = acc
    cu_vec = [cmat[(d, 0)] * u[0] + cmat[(d, 1)] * u[1] + cmat[(d, 2)] * u[2] for d in range(3)]
    ucu = u[0] * cu_vec[0] + u[1] * cu_vec[1] + u[2] * cu_vec[2]
    e_val = a_sum - 4.5 * ucu + 1.5 * a_sum * usq
    gvec = [3.0 * bvec[d] + 9.0 * cu_vec[d] - 3.0 * a_sum * u[d] for d in range(3)]
    result = []
    for j in range(19):
        r = one_b * g[j] - k[j] + e_val + b * g[OPPOSITE[j]]
        for d in range(3):
            c = VELOCITIES[j][d]
            if c > 0:
                r = r + gvec[d]
            elif c < 0:
                r = r - gvec[d]
        result.append(r)
    return result, term


def step_kernel(section, rows, g_ref, f_ref, b_ref, l_ref, res_ref, term_ref):
    planes, width_x, _ = b_ref.shape
    chunks = width_x // rows

    def body(idx, acc):
        z = idx // chunks
        x0 = pl.multiple_of((idx % chunks) * rows, rows)
        xs = pl.ds(x0, rows)
        g = [g_ref[i, z, xs, :] for i in range(19)]
        f = [f_ref[section, i, z, xs, :].astype(jnp.float32) for i in range(19)]
        b = b_ref[z, xs, :]
        lev = l_ref[z, xs, :]
        result, term = cell_math(g, f, b, lev)
        for j in range(19):
            res_ref[j, z, xs, :] = result[j]
        term_ref[xs, :] = term_ref[xs, :] + term
        return acc

    term_ref[...] = jnp.zeros_like(term_ref)
    lax.fori_loop(0, planes * chunks, body, 0)


def adjoint_step(section, pulled, forward_pops, blocking, lever):
    planes, width_x, width_y = blocking.shape
    rows = 8 if width_x % 8 == 0 else width_x
    vmem = pl.BlockSpec(memory_space=pltpu.VMEM)
    return pl.pallas_call(
        functools.partial(step_kernel, section, rows),
        out_shape=(
            jax.ShapeDtypeStruct((19, planes, width_x, width_y), jnp.float32),
            jax.ShapeDtypeStruct((width_x, width_y), jnp.float32),
        ),
        in_specs=[vmem] * 4,
        out_specs=(vmem, vmem),
    )(pulled, forward_pops, blocking, lever)


def in_grid_mask(shape, w, width_x, width_y):
    nx = lax.axis_size("gx")
    ny = lax.axis_size("gy")
    xs = lax.axis_index("gx") * width_x - w + lax.broadcasted_iota(jnp.int32, shape, 0)
    ys = lax.axis_index("gy") * width_y - w + lax.broadcasted_iota(jnp.int32, shape, 1)
    return (xs >= 0) & (xs < nx * width_x) & (ys >= 0) & (ys < ny * width_y)


def sweeps(raw_ext, valid, w):
    scale_den = 1.0 + 4.0 * FILTER_WEIGHT
    smooth = raw_ext
    for sweep in range(SWEEPS):
        framed = jnp.pad(smooth, 1)
        beside_all = framed[:-2, 1:-1] + framed[2:, 1:-1] + framed[1:-1, :-2] + framed[1:-1, 2:]
        smooth = jnp.where(valid, (raw_ext + FILTER_WEIGHT * beside_all) / scale_den, 0.0)
    return smooth[w:-w, w:-w]


def helmholtz(raw, w):
    width_x, width_y = raw.shape
    raw_ext = halo(raw, w)
    return sweeps(raw_ext, in_grid_mask(raw_ext.shape, w, width_x, width_y), w)


def pad_to(a, rows, cols):
    pad = [(0, 0)] * (a.ndim - 2) + [(0, rows - a.shape[-2]), (0, cols - a.shape[-1])]
    return jnp.pad(a, pad)


def per_device(adjoint_in, forward_pops, solid_mask, region_label, design):
    planes, width_x, width_y = solid_mask.shape
    inside = region_label > 0
    blocking = jnp.where(
        solid_mask == 1, 1.0, jnp.where(inside[None], BLOCK_LIMIT * design[None], 0.0)
    ).astype(jnp.float32)
    lever = jnp.where((solid_mask == 0) & inside[None], BLOCK_LIMIT, 0.0).astype(jnp.float32)
    saved_one = forward_pops[1].astype(jnp.float32)
    region_one = (region_label == 1).astype(jnp.float32)
    region_two = (region_label == 2).astype(jnp.float32)
    adj_ext, saved_ext, block_ext, one_ext, two_ext = halo_many(
        [adjoint_in, saved_one, blocking, region_one, region_two], [2, 1, 1, SWEEPS, SWEEPS]
    )
    valid = in_grid_mask(one_ext.shape, SWEEPS, width_x, width_y)
    weight_one = sweeps(one_ext, valid, SWEEPS)
    weight_two = sweeps(two_ext, valid, SWEEPS)
    ext_x, ext_y = width_x + 2, width_y + 2
    rows = -(-ext_x // 8) * 8
    cols = -(-ext_y // 128) * 128
    pulled = pad_to(pull_back(adj_ext, ext_x, ext_y), rows, cols)
    first, term_ext = adjoint_step(
        0,
        pulled,
        pad_to(saved_ext, rows, cols)[None],
        pad_to(block_ext, rows, cols),
        pad_to(jnp.pad(lever, ((0, 0), (1, 1), (1, 1))), rows, cols),
    )
    in_grid = in_grid_mask((ext_x, ext_y), 1, width_x, width_y)
    first = jnp.where(in_grid, first[:, :, :ext_x, :ext_y], 0.0)
    term_one = term_ext[1 : 1 + width_x, 1 : 1 + width_y]
    pulled = pull_back(first, width_x, width_y)
    adjoint, term_two = adjoint_step(0, pulled, forward_pops, blocking, lever)
    raw = SENSE_SCALE * (term_one + term_two)
    stats = jnp.stack(
        [
            jnp.sum(weight_one * raw),
            jnp.sum(weight_two * raw),
            jnp.sum(region_one),
            jnp.sum(region_two),
        ]
    )
    stats = global_sum(stats)
    smooth = helmholtz(raw, SWEEPS)
    means = stats[:2] / jnp.maximum(stats[2:], 1.0)
    sensitivity = region_one * (smooth - means[0]) + region_two * (smooth - means[1])
    return (adjoint, sensitivity)


def solution(mesh):
    in_specs = (
        P(None, None, "gx", "gy"),
        P(None, None, None, "gx", "gy"),
        P(None, "gx", "gy"),
        P("gx", "gy"),
        P("gx", "gy"),
    )
    out_specs = (P(None, None, "gx", "gy"), P("gx", "gy"))
    return jax.shard_map(
        per_device, mesh=mesh, in_specs=in_specs, out_specs=out_specs, check_vma=False
    )
```

```python
import jax
import jax.numpy as jnp
from jax import lax
from jax.sharding import PartitionSpec as P

SWEEPS = 4


VELOCITIES = [
    (0, 0, 0),
    (1, 0, 0),
    (-1, 0, 0),
    (0, 1, 0),
    (0, -1, 0),
    (0, 0, 1),
    (0, 0, -1),
    (1, 1, 0),
    (-1, -1, 0),
    (1, -1, 0),
    (-1, 1, 0),
    (1, 0, 1),
    (-1, 0, -1),
    (1, 0, -1),
    (-1, 0, 1),
    (0, 1, 1),
    (0, -1, -1),
    (0, 1, -1),
    (0, -1, 1),
]
OPPOSITE = [0, 2, 1, 4, 3, 6, 5, 8, 7, 10, 9, 12, 11, 14, 13, 16, 15, 18, 17]
WEIGHTS = [1.0 / 3.0] + [1.0 / 18.0] * 6 + [1.0 / 36.0] * 12
RELAX_RATES = [0.0] * 4 + [1.6] * 6 + [1.4] * 6 + [1.2] * 3
EXPONENTS = [
    (0, 0, 0),
    (1, 0, 0),
    (0, 1, 0),
    (0, 0, 1),
    (2, 0, 0),
    (0, 2, 0),
    (0, 0, 2),
    (1, 1, 0),
    (1, 0, 1),
    (0, 1, 1),
    (2, 1, 0),
    (2, 0, 1),
    (1, 2, 0),
    (0, 2, 1),
    (1, 0, 2),
    (0, 1, 2),
    (2, 2, 0),
    (2, 0, 2),
    (0, 2, 2),
]
BLOCK_LIMIT = 0.5
SENSE_SCALE = 20.0
FILTER_WEIGHT = 16.0

import functools

from jax.experimental import pallas as pl
from jax.experimental.pallas import tpu as pltpu

def moment_table():
    rows_out = []
    for expo in EXPONENTS:
        vector = [
            float(vel[0] ** expo[0] * vel[1] ** expo[1] * vel[2] ** expo[2]) for vel in VELOCITIES
        ]
        for prior in rows_out:
            factor = sum((a * b for a, b in zip(vector, prior))) / sum((b * b for b in prior))
            vector = [a - factor * b for a, b in zip(vector, prior)]
        rows_out.append(vector)
    norms = [sum((b * b for b in row)) for row in rows_out]
    table = []
    for first in range(19):
        line = []
        for second in range(19):
            line.append(
                sum(
                    (
                        rows_out[k][first] / norms[k] * RELAX_RATES[k] * rows_out[k][second]
                        for k in range(19)
                    )
                )
            )
        table.append(line)
    return table


RELAX = moment_table()


def halo(cells, w):
    return halo_many([cells], [w])[0]


def halo_many(arrays, widths):
    for axis, dim in (("gx", -2), ("gy", -1)):
        count = lax.axis_size(axis)
        heads, tails = [], []
        for a, w in zip(arrays, widths):
            size = a.shape[dim]
            heads.append(lax.slice_in_dim(a, 0, w, axis=a.ndim + dim))
            tails.append(lax.slice_in_dim(a, size - w, size, axis=a.ndim + dim))

        def send(pieces, pairs):
            if len(pieces) == 1:
                return [lax.ppermute(pieces[0], axis, pairs)]
            flat = jnp.concatenate([p.reshape(-1) for p in pieces])
            got = lax.ppermute(flat, axis, pairs)
            out, at = [], 0
            for p in pieces:
                out.append(got[at : at + p.size].reshape(p.shape))
                at += p.size
            return out

        lows = send(tails, [(i, i + 1) for i in range(count - 1)])
        highs = send(heads, [(i + 1, i) for i in range(count - 1)])
        arrays = [jnp.concatenate([lo, a, hi], axis=dim) for lo, a, hi in zip(lows, arrays, highs)]
    return arrays


def global_sum(values):
    ny = lax.axis_size("gy")
    bits = ny.bit_length() - 1
    assert 1 << bits == ny
    for k in range(bits):
        values = values + lax.ppermute(values, "gy", [(i, i ^ (1 << k)) for i in range(ny)])
    return lax.psum(values, "gx")


def pull_back(ext, width_x, width_y):
    pieces = []
    for slot in range(19):
        step_x, step_y, step_z = VELOCITIES[slot]
        piece = ext[slot, :, 1 + step_x : 1 + step_x + width_x, 1 + step_y : 1 + step_y + width_y]
        pieces.append(jnp.roll(piece, -step_z, axis=0))
    return jnp.stack(pieces)


def cell_math(g, f, b, lev):
    rho = f[0]
    for i in range(1, 19):
        rho = rho + f[i]
    mom = []
    for d in range(3):
        acc = None
        for i in range(19):
            c = VELOCITIES[i][d]
            if c == 0:
                continue
            acc = (f[i] if acc is None else acc + f[i]) if c > 0 else (-f[i] if acc is None else acc - f[i])
        mom.append(acc)
    u = [m / rho for m in mom]
    usq = u[0] * u[0] + u[1] * u[1] + u[2] * u[2]
    one_b = 1.0 - b
    q = []
    for j in range(19):
        acc = None
        for l in range(19):
            t = RELAX[j][l] * g[l]
            acc = t if acc is None else acc + t
        q.append(acc)
    tsum = None
    for i in range(19):
        cu = None
        for d in range(3):
            c = VELOCITIES[i][d]
            if c == 0:
                continue
            cu = (u[d] if c > 0 else -u[d]) if cu is None else (cu + u[d] if c > 0 else cu - u[d])
        if cu is None:
            phi = 1.0 - 1.5 * usq
        else:
            phi = 1.0 + 3.0 * cu + 4.5 * cu * cu - 1.5 * usq
        eq = WEIGHTS[i] * rho * phi
        t = g[i] * (f[OPPOSITE[i]] - f[i]) + q[i] * (f[i] - eq)
        tsum = t if tsum is None else tsum + t
    term = lev * tsum
    k = [one_b * qj for qj in q]
    wk = [WEIGHTS[i] * k[i] for i in range(19)]
    a_sum = wk[0]
    for i in range(1, 19):
        a_sum = a_sum + wk[i]
    bvec = []
    for d in range(3):
        acc = None
        for i in range(19):
            c = VELOCITIES[i][d]
            if c == 0:
                continue
            acc = (wk[i] if acc is None else acc + wk[i]) if c > 0 else (-wk[i] if acc is None else acc - wk[i])
        bvec.append(acc)
    cmat = {}
    for d in range(3):
        for e in range(d, 3):
            acc = None
            for i in range(19):
                c = VELOCITIES[i][d] * VELOCITIES[i][e]
                if c == 0:
                    continue
                acc = (wk[i] if acc is None else acc + wk[i]) if c > 0 else (-wk[i] if acc is None else acc - wk[i])
            cmat[(d, e)] = acc
            cmat[(e, d)] = acc
    cu_vec = [cmat[(d, 0)] * u[0] + cmat[(d, 1)] * u[1] + cmat[(d, 2)] * u[2] for d in range(3)]
    ucu = u[0] * cu_vec[0] + u[1] * cu_vec[1] + u[2] * cu_vec[2]
    e_val = a_sum - 4.5 * ucu + 1.5 * a_sum * usq
    gvec = [3.0 * bvec[d] + 9.0 * cu_vec[d] - 3.0 * a_sum * u[d] for d in range(3)]
    result = []
    for j in range(19):
        r = one_b * g[j] - k[j] + e_val + b * g[OPPOSITE[j]]
        for d in range(3):
            c = VELOCITIES[j][d]
            if c > 0:
                r = r + gvec[d]
            elif c < 0:
                r = r - gvec[d]
        result.append(r)
    return result, term


def step_kernel(section, rows, g_ref, f_ref, b_ref, l_ref, res_ref, term_ref):
    planes, width_x, _ = b_ref.shape
    chunks = width_x // rows

    def body(idx, acc):
        z = idx // chunks
        x0 = pl.multiple_of((idx % chunks) * rows, rows)
        xs = pl.ds(x0, rows)
        g = [g_ref[i, z, xs, :] for i in range(19)]
        f = [f_ref[section, i, z, xs, :].astype(jnp.float32) for i in range(19)]
        b = b_ref[z, xs, :]
        lev = l_ref[z, xs, :]
        result, term = cell_math(g, f, b, lev)
        for j in range(19):
            res_ref[j, z, xs, :] = result[j]
        term_ref[xs, :] = term_ref[xs, :] + term
        return acc

    term_ref[...] = jnp.zeros_like(term_ref)
    lax.fori_loop(0, planes * chunks, body, 0)


def adjoint_step(section, pulled, forward_pops, blocking, lever):
    planes, width_x, width_y = blocking.shape
    rows = 8 if width_x % 8 == 0 else width_x
    vmem = pl.BlockSpec(memory_space=pltpu.VMEM)
    return pl.pallas_call(
        functools.partial(step_kernel, section, rows),
        out_shape=(
            jax.ShapeDtypeStruct((19, planes, width_x, width_y), jnp.float32),
            jax.ShapeDtypeStruct((width_x, width_y), jnp.float32),
        ),
        in_specs=[vmem] * 4,
        out_specs=(vmem, vmem),
    )(pulled, forward_pops, blocking, lever)


def helmholtz(raw, w):
    scale_den = 1.0 + 4.0 * FILTER_WEIGHT
    width_x, width_y = raw.shape
    nx = lax.axis_size("gx")
    ny = lax.axis_size("gy")
    gxi = lax.axis_index("gx")
    gyi = lax.axis_index("gy")
    raw_ext = halo(raw, w)
    xs = gxi * width_x - w + lax.broadcasted_iota(jnp.int32, raw_ext.shape, 0)
    ys = gyi * width_y - w + lax.broadcasted_iota(jnp.int32, raw_ext.shape, 1)
    valid = (xs >= 0) & (xs < nx * width_x) & (ys >= 0) & (ys < ny * width_y)
    smooth = raw_ext
    for sweep in range(SWEEPS):
        framed = jnp.pad(smooth, 1)
        beside_all = framed[:-2, 1:-1] + framed[2:, 1:-1] + framed[1:-1, :-2] + framed[1:-1, 2:]
        smooth = jnp.where(valid, (raw_ext + FILTER_WEIGHT * beside_all) / scale_den, 0.0)
    return smooth[w:-w, w:-w]


def pad_to(a, rows, cols):
    pad = [(0, 0)] * (a.ndim - 2) + [(0, rows - a.shape[-2]), (0, cols - a.shape[-1])]
    return jnp.pad(a, pad)


def per_device(adjoint_in, forward_pops, solid_mask, region_label, design):
    planes, width_x, width_y = solid_mask.shape
    inside = region_label > 0
    blocking = jnp.where(
        solid_mask == 1, 1.0, jnp.where(inside[None], BLOCK_LIMIT * design[None], 0.0)
    ).astype(jnp.float32)
    lever = jnp.where((solid_mask == 0) & inside[None], BLOCK_LIMIT, 0.0).astype(jnp.float32)
    saved_one = forward_pops[1].astype(jnp.float32)
    adj_ext, saved_ext, block_ext = halo_many([adjoint_in, saved_one, blocking], [2, 1, 1])
    ext_x, ext_y = width_x + 2, width_y + 2
    rows = -(-ext_x // 8) * 8
    cols = -(-ext_y // 128) * 128
    pulled = pad_to(pull_back(adj_ext, ext_x, ext_y), rows, cols)
    first, term_ext = adjoint_step(
        0,
        pulled,
        pad_to(saved_ext, rows, cols)[None],
        pad_to(block_ext, rows, cols),
        pad_to(jnp.pad(lever, ((0, 0), (1, 1), (1, 1))), rows, cols),
    )
    gxi = lax.axis_index("gx")
    gyi = lax.axis_index("gy")
    nx = lax.axis_size("gx")
    ny = lax.axis_size("gy")
    xs = gxi * width_x - 1 + lax.broadcasted_iota(jnp.int32, (ext_x, ext_y), 0)
    ys = gyi * width_y - 1 + lax.broadcasted_iota(jnp.int32, (ext_x, ext_y), 1)
    in_grid = (xs >= 0) & (xs < nx * width_x) & (ys >= 0) & (ys < ny * width_y)
    first = jnp.where(in_grid, first[:, :, :ext_x, :ext_y], 0.0)
    term_one = term_ext[1 : 1 + width_x, 1 : 1 + width_y]
    pulled = pull_back(first, width_x, width_y)
    adjoint, term_two = adjoint_step(0, pulled, forward_pops, blocking, lever)
    raw = SENSE_SCALE * (term_one + term_two)
    smooth = helmholtz(raw, SWEEPS)
    region_one = (region_label == 1).astype(jnp.float32)
    region_two = (region_label == 2).astype(jnp.float32)
    stats = jnp.stack(
        [
            jnp.sum(smooth * region_one),
            jnp.sum(smooth * region_two),
            jnp.sum(region_one),
            jnp.sum(region_two),
        ]
    )
    stats = global_sum(stats)
    means = stats[:2] / jnp.maximum(stats[2:], 1.0)
    sensitivity = region_one * (smooth - means[0]) + region_two * (smooth - means[1])
    return (adjoint, sensitivity)


def solution(mesh):
    in_specs = (
        P(None, None, "gx", "gy"),
        P(None, None, None, "gx", "gy"),
        P(None, "gx", "gy"),
        P("gx", "gy"),
        P("gx", "gy"),
    )
    out_specs = (P(None, None, "gx", "gy"), P("gx", "gy"))
    return jax.shard_map(
        per_device, mesh=mesh, in_specs=in_specs, out_specs=out_specs, check_vma=False
    )
```

```python
import jax
import jax.numpy as jnp
from jax import lax
from jax.sharding import PartitionSpec as P

SWEEPS = 4


VELOCITIES = [
    (0, 0, 0),
    (1, 0, 0),
    (-1, 0, 0),
    (0, 1, 0),
    (0, -1, 0),
    (0, 0, 1),
    (0, 0, -1),
    (1, 1, 0),
    (-1, -1, 0),
    (1, -1, 0),
    (-1, 1, 0),
    (1, 0, 1),
    (-1, 0, -1),
    (1, 0, -1),
    (-1, 0, 1),
    (0, 1, 1),
    (0, -1, -1),
    (0, 1, -1),
    (0, -1, 1),
]
OPPOSITE = [0, 2, 1, 4, 3, 6, 5, 8, 7, 10, 9, 12, 11, 14, 13, 16, 15, 18, 17]
WEIGHTS = [1.0 / 3.0] + [1.0 / 18.0] * 6 + [1.0 / 36.0] * 12
RELAX_RATES = [0.0] * 4 + [1.6] * 6 + [1.4] * 6 + [1.2] * 3
EXPONENTS = [
    (0, 0, 0),
    (1, 0, 0),
    (0, 1, 0),
    (0, 0, 1),
    (2, 0, 0),
    (0, 2, 0),
    (0, 0, 2),
    (1, 1, 0),
    (1, 0, 1),
    (0, 1, 1),
    (2, 1, 0),
    (2, 0, 1),
    (1, 2, 0),
    (0, 2, 1),
    (1, 0, 2),
    (0, 1, 2),
    (2, 2, 0),
    (2, 0, 2),
    (0, 2, 2),
]
BLOCK_LIMIT = 0.5
SENSE_SCALE = 20.0
FILTER_WEIGHT = 16.0

import functools

from jax.experimental import pallas as pl
from jax.experimental.pallas import tpu as pltpu

def moment_table():
    rows_out = []
    for expo in EXPONENTS:
        vector = [
            float(vel[0] ** expo[0] * vel[1] ** expo[1] * vel[2] ** expo[2]) for vel in VELOCITIES
        ]
        for prior in rows_out:
            factor = sum((a * b for a, b in zip(vector, prior))) / sum((b * b for b in prior))
            vector = [a - factor * b for a, b in zip(vector, prior)]
        rows_out.append(vector)
    norms = [sum((b * b for b in row)) for row in rows_out]
    table = []
    for first in range(19):
        line = []
        for second in range(19):
            line.append(
                sum(
                    (
                        rows_out[k][first] / norms[k] * RELAX_RATES[k] * rows_out[k][second]
                        for k in range(19)
                    )
                )
            )
        table.append(line)
    return table


RELAX = moment_table()


def halo(cells, w):
    return halo_many([cells], [w])[0]


def halo_many(arrays, widths):
    for axis, dim in (("gx", -2), ("gy", -1)):
        count = lax.axis_size(axis)
        heads, tails = [], []
        for a, w in zip(arrays, widths):
            size = a.shape[dim]
            heads.append(lax.slice_in_dim(a, 0, w, axis=a.ndim + dim))
            tails.append(lax.slice_in_dim(a, size - w, size, axis=a.ndim + dim))

        def send(pieces, pairs):
            if len(pieces) == 1:
                return [lax.ppermute(pieces[0], axis, pairs)]
            flat = jnp.concatenate([p.reshape(-1) for p in pieces])
            got = lax.ppermute(flat, axis, pairs)
            out, at = [], 0
            for p in pieces:
                out.append(got[at : at + p.size].reshape(p.shape))
                at += p.size
            return out

        lows = send(tails, [(i, i + 1) for i in range(count - 1)])
        highs = send(heads, [(i + 1, i) for i in range(count - 1)])
        arrays = [jnp.concatenate([lo, a, hi], axis=dim) for lo, a, hi in zip(lows, arrays, highs)]
    return arrays


def global_sum(values):
    axes = ("gx", "gy")
    count = lax.axis_size("gx") * lax.axis_size("gy")
    rows = jnp.broadcast_to(values[None, :], (count,) + values.shape)
    return jnp.sum(lax.all_to_all(rows, axes, 0, 0, tiled=True), axis=0)


def pull_back(ext, width_x, width_y):
    pieces = []
    for slot in range(19):
        step_x, step_y, step_z = VELOCITIES[slot]
        piece = ext[slot, :, 1 + step_x : 1 + step_x + width_x, 1 + step_y : 1 + step_y + width_y]
        pieces.append(jnp.roll(piece, -step_z, axis=0))
    return jnp.stack(pieces)


def cell_math(g, f, b, lev):
    rho = f[0]
    for i in range(1, 19):
        rho = rho + f[i]
    mom = []
    for d in range(3):
        acc = None
        for i in range(19):
            c = VELOCITIES[i][d]
            if c == 0:
                continue
            acc = (f[i] if acc is None else acc + f[i]) if c > 0 else (-f[i] if acc is None else acc - f[i])
        mom.append(acc)
    u = [m / rho for m in mom]
    usq = u[0] * u[0] + u[1] * u[1] + u[2] * u[2]
    one_b = 1.0 - b
    q = []
    for j in range(19):
        acc = None
        for l in range(19):
            t = RELAX[j][l] * g[l]
            acc = t if acc is None else acc + t
        q.append(acc)
    tsum = None
    for i in range(19):
        cu = None
        for d in range(3):
            c = VELOCITIES[i][d]
            if c == 0:
                continue
            cu = (u[d] if c > 0 else -u[d]) if cu is None else (cu + u[d] if c > 0 else cu - u[d])
        if cu is None:
            phi = 1.0 - 1.5 * usq
        else:
            phi = 1.0 + 3.0 * cu + 4.5 * cu * cu - 1.5 * usq
        eq = WEIGHTS[i] * rho * phi
        t = g[i] * (f[OPPOSITE[i]] - f[i]) + q[i] * (f[i] - eq)
        tsum = t if tsum is None else tsum + t
    term = lev * tsum
    k = [one_b * qj for qj in q]
    wk = [WEIGHTS[i] * k[i] for i in range(19)]
    a_sum = wk[0]
    for i in range(1, 19):
        a_sum = a_sum + wk[i]
    bvec = []
    for d in range(3):
        acc = None
        for i in range(19):
            c = VELOCITIES[i][d]
            if c == 0:
                continue
            acc = (wk[i] if acc is None else acc + wk[i]) if c > 0 else (-wk[i] if acc is None else acc - wk[i])
        bvec.append(acc)
    cmat = {}
    for d in range(3):
        for e in range(d, 3):
            acc = None
            for i in range(19):
                c = VELOCITIES[i][d] * VELOCITIES[i][e]
                if c == 0:
                    continue
                acc = (wk[i] if acc is None else acc + wk[i]) if c > 0 else (-wk[i] if acc is None else acc - wk[i])
            cmat[(d, e)] = acc
            cmat[(e, d)] = acc
    cu_vec = [cmat[(d, 0)] * u[0] + cmat[(d, 1)] * u[1] + cmat[(d, 2)] * u[2] for d in range(3)]
    ucu = u[0] * cu_vec[0] + u[1] * cu_vec[1] + u[2] * cu_vec[2]
    e_val = a_sum - 4.5 * ucu + 1.5 * a_sum * usq
    gvec = [3.0 * bvec[d] + 9.0 * cu_vec[d] - 3.0 * a_sum * u[d] for d in range(3)]
    result = []
    for j in range(19):
        r = one_b * g[j] - k[j] + e_val + b * g[OPPOSITE[j]]
        for d in range(3):
            c = VELOCITIES[j][d]
            if c > 0:
                r = r + gvec[d]
            elif c < 0:
                r = r - gvec[d]
        result.append(r)
    return result, term


def step_kernel(section, rows, g_ref, f_ref, b_ref, l_ref, res_ref, term_ref):
    planes, width_x, _ = b_ref.shape
    chunks = width_x // rows

    def body(idx, acc):
        z = idx // chunks
        x0 = pl.multiple_of((idx % chunks) * rows, rows)
        xs = pl.ds(x0, rows)
        g = [g_ref[i, z, xs, :] for i in range(19)]
        f = [f_ref[section, i, z, xs, :].astype(jnp.float32) for i in range(19)]
        b = b_ref[z, xs, :]
        lev = l_ref[z, xs, :]
        result, term = cell_math(g, f, b, lev)
        for j in range(19):
            res_ref[j, z, xs, :] = result[j]
        term_ref[xs, :] = term_ref[xs, :] + term
        return acc

    term_ref[...] = jnp.zeros_like(term_ref)
    lax.fori_loop(0, planes * chunks, body, 0)


def adjoint_step(section, pulled, forward_pops, blocking, lever):
    planes, width_x, width_y = blocking.shape
    rows = 8 if width_x % 8 == 0 else width_x
    vmem = pl.BlockSpec(memory_space=pltpu.VMEM)
    return pl.pallas_call(
        functools.partial(step_kernel, section, rows),
        out_shape=(
            jax.ShapeDtypeStruct((19, planes, width_x, width_y), jnp.float32),
            jax.ShapeDtypeStruct((width_x, width_y), jnp.float32),
        ),
        in_specs=[vmem] * 4,
        out_specs=(vmem, vmem),
    )(pulled, forward_pops, blocking, lever)


def helmholtz(raw, w):
    scale_den = 1.0 + 4.0 * FILTER_WEIGHT
    width_x, width_y = raw.shape
    nx = lax.axis_size("gx")
    ny = lax.axis_size("gy")
    gxi = lax.axis_index("gx")
    gyi = lax.axis_index("gy")
    raw_ext = halo(raw, w)
    xs = gxi * width_x - w + lax.broadcasted_iota(jnp.int32, raw_ext.shape, 0)
    ys = gyi * width_y - w + lax.broadcasted_iota(jnp.int32, raw_ext.shape, 1)
    valid = (xs >= 0) & (xs < nx * width_x) & (ys >= 0) & (ys < ny * width_y)
    smooth = raw_ext
    for sweep in range(SWEEPS):
        framed = jnp.pad(smooth, 1)
        beside_all = framed[:-2, 1:-1] + framed[2:, 1:-1] + framed[1:-1, :-2] + framed[1:-1, 2:]
        smooth = jnp.where(valid, (raw_ext + FILTER_WEIGHT * beside_all) / scale_den, 0.0)
    return smooth[w:-w, w:-w]


def pad_to(a, rows, cols):
    pad = [(0, 0)] * (a.ndim - 2) + [(0, rows - a.shape[-2]), (0, cols - a.shape[-1])]
    return jnp.pad(a, pad)


def per_device(adjoint_in, forward_pops, solid_mask, region_label, design):
    planes, width_x, width_y = solid_mask.shape
    inside = region_label > 0
    blocking = jnp.where(
        solid_mask == 1, 1.0, jnp.where(inside[None], BLOCK_LIMIT * design[None], 0.0)
    ).astype(jnp.float32)
    lever = jnp.where((solid_mask == 0) & inside[None], BLOCK_LIMIT, 0.0).astype(jnp.float32)
    saved_one = forward_pops[1].astype(jnp.float32)
    adj_ext, saved_ext, block_ext = halo_many([adjoint_in, saved_one, blocking], [2, 1, 1])
    ext_x, ext_y = width_x + 2, width_y + 2
    rows = -(-ext_x // 8) * 8
    cols = -(-ext_y // 128) * 128
    pulled = pad_to(pull_back(adj_ext, ext_x, ext_y), rows, cols)
    first, term_ext = adjoint_step(
        0,
        pulled,
        pad_to(saved_ext, rows, cols)[None],
        pad_to(block_ext, rows, cols),
        pad_to(jnp.pad(lever, ((0, 0), (1, 1), (1, 1))), rows, cols),
    )
    gxi = lax.axis_index("gx")
    gyi = lax.axis_index("gy")
    nx = lax.axis_size("gx")
    ny = lax.axis_size("gy")
    xs = gxi * width_x - 1 + lax.broadcasted_iota(jnp.int32, (ext_x, ext_y), 0)
    ys = gyi * width_y - 1 + lax.broadcasted_iota(jnp.int32, (ext_x, ext_y), 1)
    in_grid = (xs >= 0) & (xs < nx * width_x) & (ys >= 0) & (ys < ny * width_y)
    first = jnp.where(in_grid, first[:, :, :ext_x, :ext_y], 0.0)
    term_one = term_ext[1 : 1 + width_x, 1 : 1 + width_y]
    pulled = pull_back(first, width_x, width_y)
    adjoint, term_two = adjoint_step(0, pulled, forward_pops, blocking, lever)
    raw = SENSE_SCALE * (term_one + term_two)
    smooth = helmholtz(raw, SWEEPS)
    region_one = (region_label == 1).astype(jnp.float32)
    region_two = (region_label == 2).astype(jnp.float32)
    stats = jnp.stack(
        [
            jnp.sum(smooth * region_one),
            jnp.sum(smooth * region_two),
            jnp.sum(region_one),
            jnp.sum(region_two),
        ]
    )
    stats = global_sum(stats)
    means = stats[:2] / jnp.maximum(stats[2:], 1.0)
    sensitivity = region_one * (smooth - means[0]) + region_two * (smooth - means[1])
    return (adjoint, sensitivity)


def solution(mesh):
    in_specs = (
        P(None, None, "gx", "gy"),
        P(None, None, None, "gx", "gy"),
        P(None, "gx", "gy"),
        P("gx", "gy"),
        P("gx", "gy"),
    )
    out_specs = (P(None, None, "gx", "gy"), P("gx", "gy"))
    return jax.shard_map(
        per_device, mesh=mesh, in_specs=in_specs, out_specs=out_specs, check_vma=False
    )
```

```python
import jax
import jax.numpy as jnp
from jax import lax
from jax.sharding import PartitionSpec as P

SWEEPS = 4


VELOCITIES = [
    (0, 0, 0),
    (1, 0, 0),
    (-1, 0, 0),
    (0, 1, 0),
    (0, -1, 0),
    (0, 0, 1),
    (0, 0, -1),
    (1, 1, 0),
    (-1, -1, 0),
    (1, -1, 0),
    (-1, 1, 0),
    (1, 0, 1),
    (-1, 0, -1),
    (1, 0, -1),
    (-1, 0, 1),
    (0, 1, 1),
    (0, -1, -1),
    (0, 1, -1),
    (0, -1, 1),
]
OPPOSITE = [0, 2, 1, 4, 3, 6, 5, 8, 7, 10, 9, 12, 11, 14, 13, 16, 15, 18, 17]
WEIGHTS = [1.0 / 3.0] + [1.0 / 18.0] * 6 + [1.0 / 36.0] * 12
RELAX_RATES = [0.0] * 4 + [1.6] * 6 + [1.4] * 6 + [1.2] * 3
EXPONENTS = [
    (0, 0, 0),
    (1, 0, 0),
    (0, 1, 0),
    (0, 0, 1),
    (2, 0, 0),
    (0, 2, 0),
    (0, 0, 2),
    (1, 1, 0),
    (1, 0, 1),
    (0, 1, 1),
    (2, 1, 0),
    (2, 0, 1),
    (1, 2, 0),
    (0, 2, 1),
    (1, 0, 2),
    (0, 1, 2),
    (2, 2, 0),
    (2, 0, 2),
    (0, 2, 2),
]
BLOCK_LIMIT = 0.5
SENSE_SCALE = 20.0
FILTER_WEIGHT = 16.0

import functools

from jax.experimental import pallas as pl
from jax.experimental.pallas import tpu as pltpu

def moment_table():
    rows_out = []
    for expo in EXPONENTS:
        vector = [
            float(vel[0] ** expo[0] * vel[1] ** expo[1] * vel[2] ** expo[2]) for vel in VELOCITIES
        ]
        for prior in rows_out:
            factor = sum((a * b for a, b in zip(vector, prior))) / sum((b * b for b in prior))
            vector = [a - factor * b for a, b in zip(vector, prior)]
        rows_out.append(vector)
    norms = [sum((b * b for b in row)) for row in rows_out]
    table = []
    for first in range(19):
        line = []
        for second in range(19):
            line.append(
                sum(
                    (
                        rows_out[k][first] / norms[k] * RELAX_RATES[k] * rows_out[k][second]
                        for k in range(19)
                    )
                )
            )
        table.append(line)
    return table


RELAX = moment_table()


def relax_groups():
    rows = []
    for line in RELAX:
        groups = []
        for l, value in enumerate(line):
            for group in groups:
                if abs(group[0] - value) <= 1e-12 * max(1.0, abs(value)):
                    group[1].append(l)
                    break
            else:
                groups.append((value, [l]))
        rows.append(groups)
    return rows


RELAX_GROUPS = relax_groups()


def halo(cells, w):
    return halo_many([cells], [w])[0]


def halo_many(arrays, widths):
    for axis, dim in (("gx", -2), ("gy", -1)):
        count = lax.axis_size(axis)
        heads, tails = [], []
        for a, w in zip(arrays, widths):
            size = a.shape[dim]
            heads.append(lax.slice_in_dim(a, 0, w, axis=a.ndim + dim))
            tails.append(lax.slice_in_dim(a, size - w, size, axis=a.ndim + dim))

        def send(pieces, pairs):
            if len(pieces) == 1:
                return [lax.ppermute(pieces[0], axis, pairs)]
            flat = jnp.concatenate([p.reshape(-1) for p in pieces])
            got = lax.ppermute(flat, axis, pairs)
            out, at = [], 0
            for p in pieces:
                out.append(got[at : at + p.size].reshape(p.shape))
                at += p.size
            return out

        lows = send(tails, [(i, i + 1) for i in range(count - 1)])
        highs = send(heads, [(i + 1, i) for i in range(count - 1)])
        arrays = [jnp.concatenate([lo, a, hi], axis=dim) for lo, a, hi in zip(lows, arrays, highs)]
    return arrays


def global_sum(values):
    axes = ("gx", "gy")
    count = lax.axis_size("gx") * lax.axis_size("gy")
    rows = jnp.broadcast_to(values[None, :], (count,) + values.shape)
    return jnp.sum(lax.all_to_all(rows, axes, 0, 0, tiled=True), axis=0)


def pull_back(ext, width_x, width_y):
    pieces = []
    for slot in range(19):
        step_x, step_y, step_z = VELOCITIES[slot]
        piece = ext[slot, :, 1 + step_x : 1 + step_x + width_x, 1 + step_y : 1 + step_y + width_y]
        pieces.append(jnp.roll(piece, -step_z, axis=0))
    return jnp.stack(pieces)


def cell_math(g, f, b, lev):
    rho = f[0]
    for i in range(1, 19):
        rho = rho + f[i]
    mom = []
    for d in range(3):
        acc = None
        for i in range(19):
            c = VELOCITIES[i][d]
            if c == 0:
                continue
            acc = (f[i] if acc is None else acc + f[i]) if c > 0 else (-f[i] if acc is None else acc - f[i])
        mom.append(acc)
    u = [m / rho for m in mom]
    usq = u[0] * u[0] + u[1] * u[1] + u[2] * u[2]
    one_b = 1.0 - b
    q = []
    for j in range(19):
        acc = None
        for value, members in RELAX_GROUPS[j]:
            part = g[members[0]]
            for l in members[1:]:
                part = part + g[l]
            t = value * part
            acc = t if acc is None else acc + t
        q.append(acc)
    tsum = None
    for i in range(19):
        cu = None
        for d in range(3):
            c = VELOCITIES[i][d]
            if c == 0:
                continue
            cu = (u[d] if c > 0 else -u[d]) if cu is None else (cu + u[d] if c > 0 else cu - u[d])
        if cu is None:
            phi = 1.0 - 1.5 * usq
        else:
            phi = 1.0 + 3.0 * cu + 4.5 * cu * cu - 1.5 * usq
        eq = WEIGHTS[i] * rho * phi
        t = g[i] * (f[OPPOSITE[i]] - f[i]) + q[i] * (f[i] - eq)
        tsum = t if tsum is None else tsum + t
    term = lev * tsum
    k = [one_b * qj for qj in q]
    wk = [WEIGHTS[i] * k[i] for i in range(19)]
    a_sum = wk[0]
    for i in range(1, 19):
        a_sum = a_sum + wk[i]
    bvec = []
    for d in range(3):
        acc = None
        for i in range(19):
            c = VELOCITIES[i][d]
            if c == 0:
                continue
            acc = (wk[i] if acc is None else acc + wk[i]) if c > 0 else (-wk[i] if acc is None else acc - wk[i])
        bvec.append(acc)
    cmat = {}
    for d in range(3):
        for e in range(d, 3):
            acc = None
            for i in range(19):
                c = VELOCITIES[i][d] * VELOCITIES[i][e]
                if c == 0:
                    continue
                acc = (wk[i] if acc is None else acc + wk[i]) if c > 0 else (-wk[i] if acc is None else acc - wk[i])
            cmat[(d, e)] = acc
            cmat[(e, d)] = acc
    cu_vec = [cmat[(d, 0)] * u[0] + cmat[(d, 1)] * u[1] + cmat[(d, 2)] * u[2] for d in range(3)]
    ucu = u[0] * cu_vec[0] + u[1] * cu_vec[1] + u[2] * cu_vec[2]
    e_val = a_sum - 4.5 * ucu + 1.5 * a_sum * usq
    gvec = [3.0 * bvec[d] + 9.0 * cu_vec[d] - 3.0 * a_sum * u[d] for d in range(3)]
    result = []
    for j in range(19):
        r = one_b * g[j] - k[j] + e_val + b * g[OPPOSITE[j]]
        for d in range(3):
            c = VELOCITIES[j][d]
            if c > 0:
                r = r + gvec[d]
            elif c < 0:
                r = r - gvec[d]
        result.append(r)
    return result, term


def step_kernel(section, rows, g_ref, f_ref, b_ref, l_ref, res_ref, term_ref):
    planes, width_x, _ = b_ref.shape
    chunks = width_x // rows

    def body(idx, acc):
        z = idx // chunks
        x0 = pl.multiple_of((idx % chunks) * rows, rows)
        xs = pl.ds(x0, rows)
        g = [g_ref[i, z, xs, :] for i in range(19)]
        f = [f_ref[section, i, z, xs, :].astype(jnp.float32) for i in range(19)]
        b = b_ref[z, xs, :]
        lev = l_ref[z, xs, :]
        result, term = cell_math(g, f, b, lev)
        for j in range(19):
            res_ref[j, z, xs, :] = result[j]
        term_ref[xs, :] = term_ref[xs, :] + term
        return acc

    term_ref[...] = jnp.zeros_like(term_ref)
    lax.fori_loop(0, planes * chunks, body, 0)


def adjoint_step(section, pulled, forward_pops, blocking, lever):
    planes, width_x, width_y = blocking.shape
    rows = 8 if width_x % 8 == 0 else width_x
    vmem = pl.BlockSpec(memory_space=pltpu.VMEM)
    return pl.pallas_call(
        functools.partial(step_kernel, section, rows),
        out_shape=(
            jax.ShapeDtypeStruct((19, planes, width_x, width_y), jnp.float32),
            jax.ShapeDtypeStruct((width_x, width_y), jnp.float32),
        ),
        in_specs=[vmem] * 4,
        out_specs=(vmem, vmem),
    )(pulled, forward_pops, blocking, lever)


def helmholtz(raw, w):
    scale_den = 1.0 + 4.0 * FILTER_WEIGHT
    width_x, width_y = raw.shape
    nx = lax.axis_size("gx")
    ny = lax.axis_size("gy")
    gxi = lax.axis_index("gx")
    gyi = lax.axis_index("gy")
    raw_ext = halo(raw, w)
    xs = gxi * width_x - w + lax.broadcasted_iota(jnp.int32, raw_ext.shape, 0)
    ys = gyi * width_y - w + lax.broadcasted_iota(jnp.int32, raw_ext.shape, 1)
    valid = (xs >= 0) & (xs < nx * width_x) & (ys >= 0) & (ys < ny * width_y)
    smooth = raw_ext
    for sweep in range(SWEEPS):
        framed = jnp.pad(smooth, 1)
        beside_all = framed[:-2, 1:-1] + framed[2:, 1:-1] + framed[1:-1, :-2] + framed[1:-1, 2:]
        smooth = jnp.where(valid, (raw_ext + FILTER_WEIGHT * beside_all) / scale_den, 0.0)
    return smooth[w:-w, w:-w]


def pad_to(a, rows, cols):
    pad = [(0, 0)] * (a.ndim - 2) + [(0, rows - a.shape[-2]), (0, cols - a.shape[-1])]
    return jnp.pad(a, pad)


def per_device(adjoint_in, forward_pops, solid_mask, region_label, design):
    planes, width_x, width_y = solid_mask.shape
    inside = region_label > 0
    blocking = jnp.where(
        solid_mask == 1, 1.0, jnp.where(inside[None], BLOCK_LIMIT * design[None], 0.0)
    ).astype(jnp.float32)
    lever = jnp.where((solid_mask == 0) & inside[None], BLOCK_LIMIT, 0.0).astype(jnp.float32)
    saved_one = forward_pops[1].astype(jnp.float32)
    adj_ext, saved_ext, block_ext = halo_many([adjoint_in, saved_one, blocking], [2, 1, 1])
    ext_x, ext_y = width_x + 2, width_y + 2
    rows = -(-ext_x // 8) * 8
    cols = -(-ext_y // 128) * 128
    pulled = pad_to(pull_back(adj_ext, ext_x, ext_y), rows, cols)
    first, term_ext = adjoint_step(
        0,
        pulled,
        pad_to(saved_ext, rows, cols).astype(jnp.bfloat16)[None],
        pad_to(block_ext, rows, cols),
        pad_to(jnp.pad(lever, ((0, 0), (1, 1), (1, 1))), rows, cols),
    )
    gxi = lax.axis_index("gx")
    gyi = lax.axis_index("gy")
    nx = lax.axis_size("gx")
    ny = lax.axis_size("gy")
    xs = gxi * width_x - 1 + lax.broadcasted_iota(jnp.int32, (ext_x, ext_y), 0)
    ys = gyi * width_y - 1 + lax.broadcasted_iota(jnp.int32, (ext_x, ext_y), 1)
    in_grid = (xs >= 0) & (xs < nx * width_x) & (ys >= 0) & (ys < ny * width_y)
    first = jnp.where(in_grid, first[:, :, :ext_x, :ext_y], 0.0)
    term_one = term_ext[1 : 1 + width_x, 1 : 1 + width_y]
    pulled = pull_back(first, width_x, width_y)
    adjoint, term_two = adjoint_step(0, pulled, forward_pops, blocking, lever)
    raw = SENSE_SCALE * (term_one + term_two)
    smooth = helmholtz(raw, SWEEPS)
    region_one = (region_label == 1).astype(jnp.float32)
    region_two = (region_label == 2).astype(jnp.float32)
    stats = jnp.stack(
        [
            jnp.sum(smooth * region_one),
            jnp.sum(smooth * region_two),
            jnp.sum(region_one),
            jnp.sum(region_two),
        ]
    )
    stats = global_sum(stats)
    means = stats[:2] / jnp.maximum(stats[2:], 1.0)
    sensitivity = region_one * (smooth - means[0]) + region_two * (smooth - means[1])
    return (adjoint, sensitivity)


def solution(mesh):
    in_specs = (
        P(None, None, "gx", "gy"),
        P(None, None, None, "gx", "gy"),
        P(None, "gx", "gy"),
        P("gx", "gy"),
        P("gx", "gy"),
    )
    out_specs = (P(None, None, "gx", "gy"), P("gx", "gy"))
    return jax.shard_map(
        per_device, mesh=mesh, in_specs=in_specs, out_specs=out_specs, check_vma=False
    )
```

```python
import jax
import jax.numpy as jnp
from jax import lax
from jax.sharding import PartitionSpec as P

SWEEPS = 4


VELOCITIES = [
    (0, 0, 0),
    (1, 0, 0),
    (-1, 0, 0),
    (0, 1, 0),
    (0, -1, 0),
    (0, 0, 1),
    (0, 0, -1),
    (1, 1, 0),
    (-1, -1, 0),
    (1, -1, 0),
    (-1, 1, 0),
    (1, 0, 1),
    (-1, 0, -1),
    (1, 0, -1),
    (-1, 0, 1),
    (0, 1, 1),
    (0, -1, -1),
    (0, 1, -1),
    (0, -1, 1),
]
OPPOSITE = [0, 2, 1, 4, 3, 6, 5, 8, 7, 10, 9, 12, 11, 14, 13, 16, 15, 18, 17]
WEIGHTS = [1.0 / 3.0] + [1.0 / 18.0] * 6 + [1.0 / 36.0] * 12
RELAX_RATES = [0.0] * 4 + [1.6] * 6 + [1.4] * 6 + [1.2] * 3
EXPONENTS = [
    (0, 0, 0),
    (1, 0, 0),
    (0, 1, 0),
    (0, 0, 1),
    (2, 0, 0),
    (0, 2, 0),
    (0, 0, 2),
    (1, 1, 0),
    (1, 0, 1),
    (0, 1, 1),
    (2, 1, 0),
    (2, 0, 1),
    (1, 2, 0),
    (0, 2, 1),
    (1, 0, 2),
    (0, 1, 2),
    (2, 2, 0),
    (2, 0, 2),
    (0, 2, 2),
]
BLOCK_LIMIT = 0.5
SENSE_SCALE = 20.0
FILTER_WEIGHT = 16.0

import functools

from jax.experimental import pallas as pl
from jax.experimental.pallas import tpu as pltpu

def moment_table():
    rows_out = []
    for expo in EXPONENTS:
        vector = [
            float(vel[0] ** expo[0] * vel[1] ** expo[1] * vel[2] ** expo[2]) for vel in VELOCITIES
        ]
        for prior in rows_out:
            factor = sum((a * b for a, b in zip(vector, prior))) / sum((b * b for b in prior))
            vector = [a - factor * b for a, b in zip(vector, prior)]
        rows_out.append(vector)
    norms = [sum((b * b for b in row)) for row in rows_out]
    table = []
    for first in range(19):
        line = []
        for second in range(19):
            line.append(
                sum(
                    (
                        rows_out[k][first] / norms[k] * RELAX_RATES[k] * rows_out[k][second]
                        for k in range(19)
                    )
                )
            )
        table.append(line)
    return table


RELAX = moment_table()


def relax_groups():
    rows = []
    for line in RELAX:
        groups = []
        for l, value in enumerate(line):
            for group in groups:
                if abs(group[0] - value) <= 1e-12 * max(1.0, abs(value)):
                    group[1].append(l)
                    break
            else:
                groups.append((value, [l]))
        rows.append(groups)
    return rows


RELAX_GROUPS = relax_groups()


def halo(cells, w):
    return halo_many([cells], [w])[0]


def halo_many(arrays, widths):
    for axis, dim in (("gx", -2), ("gy", -1)):
        count = lax.axis_size(axis)
        heads, tails = [], []
        for a, w in zip(arrays, widths):
            size = a.shape[dim]
            heads.append(lax.slice_in_dim(a, 0, w, axis=a.ndim + dim))
            tails.append(lax.slice_in_dim(a, size - w, size, axis=a.ndim + dim))

        def send(pieces, pairs):
            if len(pieces) == 1:
                got = lax.ppermute(pieces[0].astype(jnp.float32), axis, pairs)
                return [got.astype(pieces[0].dtype)]
            flat = jnp.concatenate([p.astype(jnp.float32).reshape(-1) for p in pieces])
            got = lax.ppermute(flat, axis, pairs)
            out, at = [], 0
            for p in pieces:
                out.append(got[at : at + p.size].reshape(p.shape).astype(p.dtype))
                at += p.size
            return out

        lows = send(tails, [(i, i + 1) for i in range(count - 1)])
        highs = send(heads, [(i + 1, i) for i in range(count - 1)])
        arrays = [jnp.concatenate([lo, a, hi], axis=dim) for lo, a, hi in zip(lows, arrays, highs)]
    return arrays


def global_sum(values):
    axes = ("gx", "gy")
    count = lax.axis_size("gx") * lax.axis_size("gy")
    rows = jnp.broadcast_to(values[None, :], (count,) + values.shape)
    return jnp.sum(lax.all_to_all(rows, axes, 0, 0, tiled=True), axis=0)


def pull_back(ext, width_x, width_y):
    pieces = []
    for slot in range(19):
        step_x, step_y, step_z = VELOCITIES[slot]
        piece = ext[slot, :, 1 + step_x : 1 + step_x + width_x, 1 + step_y : 1 + step_y + width_y]
        pieces.append(jnp.roll(piece, -step_z, axis=0))
    return jnp.stack(pieces)


def cell_math(g, f, b, lev):
    rho = f[0]
    for i in range(1, 19):
        rho = rho + f[i]
    mom = []
    for d in range(3):
        acc = None
        for i in range(19):
            c = VELOCITIES[i][d]
            if c == 0:
                continue
            acc = (f[i] if acc is None else acc + f[i]) if c > 0 else (-f[i] if acc is None else acc - f[i])
        mom.append(acc)
    u = [m / rho for m in mom]
    usq = u[0] * u[0] + u[1] * u[1] + u[2] * u[2]
    one_b = 1.0 - b
    q = []
    for j in range(19):
        acc = None
        for value, members in RELAX_GROUPS[j]:
            part = g[members[0]]
            for l in members[1:]:
                part = part + g[l]
            t = value * part
            acc = t if acc is None else acc + t
        q.append(acc)
    tsum = None
    for i in range(19):
        cu = None
        for d in range(3):
            c = VELOCITIES[i][d]
            if c == 0:
                continue
            cu = (u[d] if c > 0 else -u[d]) if cu is None else (cu + u[d] if c > 0 else cu - u[d])
        if cu is None:
            phi = 1.0 - 1.5 * usq
        else:
            phi = 1.0 + 3.0 * cu + 4.5 * cu * cu - 1.5 * usq
        eq = WEIGHTS[i] * rho * phi
        t = g[i] * (f[OPPOSITE[i]] - f[i]) + q[i] * (f[i] - eq)
        tsum = t if tsum is None else tsum + t
    term = lev * tsum
    k = [one_b * qj for qj in q]
    wk = [WEIGHTS[i] * k[i] for i in range(19)]
    a_sum = wk[0]
    for i in range(1, 19):
        a_sum = a_sum + wk[i]
    bvec = []
    for d in range(3):
        acc = None
        for i in range(19):
            c = VELOCITIES[i][d]
            if c == 0:
                continue
            acc = (wk[i] if acc is None else acc + wk[i]) if c > 0 else (-wk[i] if acc is None else acc - wk[i])
        bvec.append(acc)
    cmat = {}
    for d in range(3):
        for e in range(d, 3):
            acc = None
            for i in range(19):
                c = VELOCITIES[i][d] * VELOCITIES[i][e]
                if c == 0:
                    continue
                acc = (wk[i] if acc is None else acc + wk[i]) if c > 0 else (-wk[i] if acc is None else acc - wk[i])
            cmat[(d, e)] = acc
            cmat[(e, d)] = acc
    cu_vec = [cmat[(d, 0)] * u[0] + cmat[(d, 1)] * u[1] + cmat[(d, 2)] * u[2] for d in range(3)]
    ucu = u[0] * cu_vec[0] + u[1] * cu_vec[1] + u[2] * cu_vec[2]
    e_val = a_sum - 4.5 * ucu + 1.5 * a_sum * usq
    gvec = [3.0 * bvec[d] + 9.0 * cu_vec[d] - 3.0 * a_sum * u[d] for d in range(3)]
    result = []
    for j in range(19):
        r = one_b * g[j] - k[j] + e_val + b * g[OPPOSITE[j]]
        for d in range(3):
            c = VELOCITIES[j][d]
            if c > 0:
                r = r + gvec[d]
            elif c < 0:
                r = r - gvec[d]
        result.append(r)
    return result, term


def step_kernel(section, rows, g_ref, f_ref, b_ref, l_ref, res_ref, term_ref):
    planes, width_x, _ = b_ref.shape
    chunks = width_x // rows

    def body(idx, acc):
        z = idx // chunks
        x0 = pl.multiple_of((idx % chunks) * rows, rows)
        xs = pl.ds(x0, rows)
        g = [g_ref[i, z, xs, :] for i in range(19)]
        f = [f_ref[section, i, z, xs, :].astype(jnp.float32) for i in range(19)]
        b = b_ref[z, xs, :]
        lev = l_ref[z, xs, :]
        result, term = cell_math(g, f, b, lev)
        for j in range(19):
            res_ref[j, z, xs, :] = result[j]
        term_ref[xs, :] = term_ref[xs, :] + term
        return acc

    term_ref[...] = jnp.zeros_like(term_ref)
    lax.fori_loop(0, planes * chunks, body, 0)


def adjoint_step(section, pulled, forward_pops, blocking, lever):
    planes, width_x, width_y = blocking.shape
    rows = 8 if width_x % 8 == 0 else width_x
    vmem = pl.BlockSpec(memory_space=pltpu.VMEM)
    return pl.pallas_call(
        functools.partial(step_kernel, section, rows),
        out_shape=(
            jax.ShapeDtypeStruct((19, planes, width_x, width_y), jnp.float32),
            jax.ShapeDtypeStruct((width_x, width_y), jnp.float32),
        ),
        in_specs=[vmem] * 4,
        out_specs=(vmem, vmem),
    )(pulled, forward_pops, blocking, lever)


def helmholtz(raw, w):
    scale_den = 1.0 + 4.0 * FILTER_WEIGHT
    width_x, width_y = raw.shape
    nx = lax.axis_size("gx")
    ny = lax.axis_size("gy")
    gxi = lax.axis_index("gx")
    gyi = lax.axis_index("gy")
    raw_ext = halo(raw, w)
    xs = gxi * width_x - w + lax.broadcasted_iota(jnp.int32, raw_ext.shape, 0)
    ys = gyi * width_y - w + lax.broadcasted_iota(jnp.int32, raw_ext.shape, 1)
    valid = (xs >= 0) & (xs < nx * width_x) & (ys >= 0) & (ys < ny * width_y)
    smooth = raw_ext
    for sweep in range(SWEEPS):
        framed = jnp.pad(smooth, 1)
        beside_all = framed[:-2, 1:-1] + framed[2:, 1:-1] + framed[1:-1, :-2] + framed[1:-1, 2:]
        smooth = jnp.where(valid, (raw_ext + FILTER_WEIGHT * beside_all) / scale_den, 0.0)
    return smooth[w:-w, w:-w]


def pad_to(a, rows, cols):
    pad = [(0, 0)] * (a.ndim - 2) + [(0, rows - a.shape[-2]), (0, cols - a.shape[-1])]
    return jnp.pad(a, pad)


def per_device(adjoint_in, forward_pops, solid_mask, region_label, design):
    planes, width_x, width_y = solid_mask.shape
    inside = region_label > 0
    blocking = jnp.where(
        solid_mask == 1, 1.0, jnp.where(inside[None], BLOCK_LIMIT * design[None], 0.0)
    ).astype(jnp.float32)
    lever = jnp.where((solid_mask == 0) & inside[None], BLOCK_LIMIT, 0.0).astype(jnp.float32)
    saved_one = forward_pops[1]
    adj_ext, saved_ext, block_ext = halo_many([adjoint_in, saved_one, blocking], [2, 1, 1])
    ext_x, ext_y = width_x + 2, width_y + 2
    rows = -(-ext_x // 8) * 8
    cols = -(-ext_y // 128) * 128
    pulled = pad_to(pull_back(adj_ext, ext_x, ext_y), rows, cols)
    first, term_ext = adjoint_step(
        0,
        pulled,
        pad_to(saved_ext, rows, cols)[None],
        pad_to(block_ext, rows, cols),
        pad_to(jnp.pad(lever, ((0, 0), (1, 1), (1, 1))), rows, cols),
    )
    gxi = lax.axis_index("gx")
    gyi = lax.axis_index("gy")
    nx = lax.axis_size("gx")
    ny = lax.axis_size("gy")
    xs = gxi * width_x - 1 + lax.broadcasted_iota(jnp.int32, (ext_x, ext_y), 0)
    ys = gyi * width_y - 1 + lax.broadcasted_iota(jnp.int32, (ext_x, ext_y), 1)
    in_grid = (xs >= 0) & (xs < nx * width_x) & (ys >= 0) & (ys < ny * width_y)
    first = jnp.where(in_grid, first[:, :, :ext_x, :ext_y], 0.0)
    term_one = term_ext[1 : 1 + width_x, 1 : 1 + width_y]
    pulled = pull_back(first, width_x, width_y)
    adjoint, term_two = adjoint_step(0, pulled, forward_pops, blocking, lever)
    raw = SENSE_SCALE * (term_one + term_two)
    smooth = helmholtz(raw, SWEEPS)
    region_one = (region_label == 1).astype(jnp.float32)
    region_two = (region_label == 2).astype(jnp.float32)
    stats = jnp.stack(
        [
            jnp.sum(smooth * region_one),
            jnp.sum(smooth * region_two),
            jnp.sum(region_one),
            jnp.sum(region_two),
        ]
    )
    stats = global_sum(stats)
    means = stats[:2] / jnp.maximum(stats[2:], 1.0)
    sensitivity = region_one * (smooth - means[0]) + region_two * (smooth - means[1])
    return (adjoint, sensitivity)


def solution(mesh):
    in_specs = (
        P(None, None, "gx", "gy"),
        P(None, None, None, "gx", "gy"),
        P(None, "gx", "gy"),
        P("gx", "gy"),
        P("gx", "gy"),
    )
    out_specs = (P(None, None, "gx", "gy"), P("gx", "gy"))
    return jax.shard_map(
        per_device, mesh=mesh, in_specs=in_specs, out_specs=out_specs, check_vma=False
    )
```

```python
import jax
import jax.numpy as jnp
from jax import lax
from jax.sharding import PartitionSpec as P

SWEEPS = 4


VELOCITIES = [
    (0, 0, 0),
    (1, 0, 0),
    (-1, 0, 0),
    (0, 1, 0),
    (0, -1, 0),
    (0, 0, 1),
    (0, 0, -1),
    (1, 1, 0),
    (-1, -1, 0),
    (1, -1, 0),
    (-1, 1, 0),
    (1, 0, 1),
    (-1, 0, -1),
    (1, 0, -1),
    (-1, 0, 1),
    (0, 1, 1),
    (0, -1, -1),
    (0, 1, -1),
    (0, -1, 1),
]
OPPOSITE = [0, 2, 1, 4, 3, 6, 5, 8, 7, 10, 9, 12, 11, 14, 13, 16, 15, 18, 17]
WEIGHTS = [1.0 / 3.0] + [1.0 / 18.0] * 6 + [1.0 / 36.0] * 12
RELAX_RATES = [0.0] * 4 + [1.6] * 6 + [1.4] * 6 + [1.2] * 3
EXPONENTS = [
    (0, 0, 0),
    (1, 0, 0),
    (0, 1, 0),
    (0, 0, 1),
    (2, 0, 0),
    (0, 2, 0),
    (0, 0, 2),
    (1, 1, 0),
    (1, 0, 1),
    (0, 1, 1),
    (2, 1, 0),
    (2, 0, 1),
    (1, 2, 0),
    (0, 2, 1),
    (1, 0, 2),
    (0, 1, 2),
    (2, 2, 0),
    (2, 0, 2),
    (0, 2, 2),
]
BLOCK_LIMIT = 0.5
SENSE_SCALE = 20.0
FILTER_WEIGHT = 16.0

import functools

from jax.experimental import pallas as pl
from jax.experimental.pallas import tpu as pltpu

def moment_table():
    rows_out = []
    for expo in EXPONENTS:
        vector = [
            float(vel[0] ** expo[0] * vel[1] ** expo[1] * vel[2] ** expo[2]) for vel in VELOCITIES
        ]
        for prior in rows_out:
            factor = sum((a * b for a, b in zip(vector, prior))) / sum((b * b for b in prior))
            vector = [a - factor * b for a, b in zip(vector, prior)]
        rows_out.append(vector)
    norms = [sum((b * b for b in row)) for row in rows_out]
    table = []
    for first in range(19):
        line = []
        for second in range(19):
            line.append(
                sum(
                    (
                        rows_out[k][first] / norms[k] * RELAX_RATES[k] * rows_out[k][second]
                        for k in range(19)
                    )
                )
            )
        table.append(line)
    return table


RELAX = moment_table()


def relax_groups():
    rows = []
    for line in RELAX:
        groups = []
        for l, value in enumerate(line):
            for group in groups:
                if abs(group[0] - value) <= 1e-12 * max(1.0, abs(value)):
                    group[1].append(l)
                    break
            else:
                groups.append((value, [l]))
        rows.append(groups)
    return rows


RELAX_GROUPS = relax_groups()


def halo(cells, w):
    return halo_many([cells], [w])[0]


def halo_many(arrays, widths):
    for axis, dim in (("gx", -2), ("gy", -1)):
        count = lax.axis_size(axis)
        heads, tails = [], []
        for a, w in zip(arrays, widths):
            size = a.shape[dim]
            heads.append(lax.slice_in_dim(a, 0, w, axis=a.ndim + dim))
            tails.append(lax.slice_in_dim(a, size - w, size, axis=a.ndim + dim))

        def send(pieces, pairs):
            if len(pieces) == 1:
                got = lax.ppermute(pieces[0].astype(jnp.float32), axis, pairs)
                return [got.astype(pieces[0].dtype)]
            flat = jnp.concatenate([p.astype(jnp.float32).reshape(-1) for p in pieces])
            got = lax.ppermute(flat, axis, pairs)
            out, at = [], 0
            for p in pieces:
                out.append(got[at : at + p.size].reshape(p.shape).astype(p.dtype))
                at += p.size
            return out

        lows = send(tails, [(i, i + 1) for i in range(count - 1)])
        highs = send(heads, [(i + 1, i) for i in range(count - 1)])
        arrays = [jnp.concatenate([lo, a, hi], axis=dim) for lo, a, hi in zip(lows, arrays, highs)]
    return arrays


def global_sum(values):
    axes = ("gx", "gy")
    count = lax.axis_size("gx") * lax.axis_size("gy")
    rows = jnp.broadcast_to(values[None, :], (count,) + values.shape)
    return jnp.sum(lax.all_to_all(rows, axes, 0, 0, tiled=True), axis=0)


def pull_back(ext, width_x, width_y):
    pieces = []
    for slot in range(19):
        step_x, step_y, step_z = VELOCITIES[slot]
        piece = ext[slot, :, 1 + step_x : 1 + step_x + width_x, 1 + step_y : 1 + step_y + width_y]
        pieces.append(jnp.roll(piece, -step_z, axis=0))
    return jnp.stack(pieces)


def cell_math(g, f, b, lev):
    rho = f[0]
    for i in range(1, 19):
        rho = rho + f[i]
    mom = []
    for d in range(3):
        acc = None
        for i in range(19):
            c = VELOCITIES[i][d]
            if c == 0:
                continue
            acc = (f[i] if acc is None else acc + f[i]) if c > 0 else (-f[i] if acc is None else acc - f[i])
        mom.append(acc)
    u = [m / rho for m in mom]
    usq = u[0] * u[0] + u[1] * u[1] + u[2] * u[2]
    one_b = 1.0 - b
    q = []
    for j in range(19):
        acc = None
        for value, members in RELAX_GROUPS[j]:
            part = g[members[0]]
            for l in members[1:]:
                part = part + g[l]
            t = value * part
            acc = t if acc is None else acc + t
        q.append(acc)
    tsum = None
    for i in range(19):
        cu = None
        for d in range(3):
            c = VELOCITIES[i][d]
            if c == 0:
                continue
            cu = (u[d] if c > 0 else -u[d]) if cu is None else (cu + u[d] if c > 0 else cu - u[d])
        if cu is None:
            phi = 1.0 - 1.5 * usq
        else:
            phi = 1.0 + 3.0 * cu + 4.5 * cu * cu - 1.5 * usq
        eq = WEIGHTS[i] * rho * phi
        t = g[i] * (f[OPPOSITE[i]] - f[i]) + q[i] * (f[i] - eq)
        tsum = t if tsum is None else tsum + t
    term = lev * tsum
    k = [one_b * qj for qj in q]
    wk = [WEIGHTS[i] * k[i] for i in range(19)]
    a_sum = wk[0]
    for i in range(1, 19):
        a_sum = a_sum + wk[i]
    bvec = []
    for d in range(3):
        acc = None
        for i in range(19):
            c = VELOCITIES[i][d]
            if c == 0:
                continue
            acc = (wk[i] if acc is None else acc + wk[i]) if c > 0 else (-wk[i] if acc is None else acc - wk[i])
        bvec.append(acc)
    cmat = {}
    for d in range(3):
        for e in range(d, 3):
            acc = None
            for i in range(19):
                c = VELOCITIES[i][d] * VELOCITIES[i][e]
                if c == 0:
                    continue
                acc = (wk[i] if acc is None else acc + wk[i]) if c > 0 else (-wk[i] if acc is None else acc - wk[i])
            cmat[(d, e)] = acc
            cmat[(e, d)] = acc
    cu_vec = [cmat[(d, 0)] * u[0] + cmat[(d, 1)] * u[1] + cmat[(d, 2)] * u[2] for d in range(3)]
    ucu = u[0] * cu_vec[0] + u[1] * cu_vec[1] + u[2] * cu_vec[2]
    e_val = a_sum - 4.5 * ucu + 1.5 * a_sum * usq
    gvec = [3.0 * bvec[d] + 9.0 * cu_vec[d] - 3.0 * a_sum * u[d] for d in range(3)]
    result = []
    for j in range(19):
        r = one_b * g[j] - k[j] + e_val + b * g[OPPOSITE[j]]
        for d in range(3):
            c = VELOCITIES[j][d]
            if c > 0:
                r = r + gvec[d]
            elif c < 0:
                r = r - gvec[d]
        result.append(r)
    return result, term


def step_kernel(section, rows, g_ref, f_ref, b_ref, l_ref, res_ref, term_ref):
    planes, width_x, _ = b_ref.shape
    chunks = width_x // rows

    def body(idx, acc):
        z = idx // chunks
        x0 = pl.multiple_of((idx % chunks) * rows, rows)
        xs = pl.ds(x0, rows)
        g = [g_ref[i, z, xs, :] for i in range(19)]
        f = [f_ref[section, i, z, xs, :].astype(jnp.float32) for i in range(19)]
        b = b_ref[z, xs, :]
        lev = l_ref[z, xs, :]
        result, term = cell_math(g, f, b, lev)
        for j in range(19):
            res_ref[j, z, xs, :] = result[j]
        term_ref[xs, :] = term_ref[xs, :] + term
        return acc

    term_ref[...] = jnp.zeros_like(term_ref)
    lax.fori_loop(0, planes * chunks, body, 0)


def adjoint_step(section, pulled, forward_pops, blocking, lever):
    planes, width_x, width_y = blocking.shape
    rows = max(8, 2048 // width_y)
    if width_x % rows:
        rows = 8 if width_x % 8 == 0 else width_x
    vmem = pl.BlockSpec(memory_space=pltpu.VMEM)
    return pl.pallas_call(
        functools.partial(step_kernel, section, rows),
        out_shape=(
            jax.ShapeDtypeStruct((19, planes, width_x, width_y), jnp.float32),
            jax.ShapeDtypeStruct((width_x, width_y), jnp.float32),
        ),
        in_specs=[vmem] * 4,
        out_specs=(vmem, vmem),
    )(pulled, forward_pops, blocking, lever)


def helmholtz(raw, w):
    scale_den = 1.0 + 4.0 * FILTER_WEIGHT
    width_x, width_y = raw.shape
    nx = lax.axis_size("gx")
    ny = lax.axis_size("gy")
    gxi = lax.axis_index("gx")
    gyi = lax.axis_index("gy")
    raw_ext = halo(raw, w)
    xs = gxi * width_x - w + lax.broadcasted_iota(jnp.int32, raw_ext.shape, 0)
    ys = gyi * width_y - w + lax.broadcasted_iota(jnp.int32, raw_ext.shape, 1)
    valid = (xs >= 0) & (xs < nx * width_x) & (ys >= 0) & (ys < ny * width_y)
    smooth = raw_ext
    for sweep in range(SWEEPS):
        framed = jnp.pad(smooth, 1)
        beside_all = framed[:-2, 1:-1] + framed[2:, 1:-1] + framed[1:-1, :-2] + framed[1:-1, 2:]
        smooth = jnp.where(valid, (raw_ext + FILTER_WEIGHT * beside_all) / scale_den, 0.0)
    return smooth[w:-w, w:-w]


def pad_to(a, rows, cols):
    pad = [(0, 0)] * (a.ndim - 2) + [(0, rows - a.shape[-2]), (0, cols - a.shape[-1])]
    return jnp.pad(a, pad)


def per_device(adjoint_in, forward_pops, solid_mask, region_label, design):
    planes, width_x, width_y = solid_mask.shape
    inside = region_label > 0
    blocking = jnp.where(
        solid_mask == 1, 1.0, jnp.where(inside[None], BLOCK_LIMIT * design[None], 0.0)
    ).astype(jnp.float32)
    lever = jnp.where((solid_mask == 0) & inside[None], BLOCK_LIMIT, 0.0).astype(jnp.float32)
    saved_one = forward_pops[1]
    adj_ext, saved_ext, block_ext = halo_many([adjoint_in, saved_one, blocking], [2, 1, 1])
    ext_x, ext_y = width_x + 2, width_y + 2
    rows = -(-ext_x // 8) * 8
    cols = -(-ext_y // 128) * 128
    pulled = pad_to(pull_back(adj_ext, ext_x, ext_y), rows, cols)
    first, term_ext = adjoint_step(
        0,
        pulled,
        pad_to(saved_ext, rows, cols)[None],
        pad_to(block_ext, rows, cols),
        pad_to(jnp.pad(lever, ((0, 0), (1, 1), (1, 1))), rows, cols),
    )
    gxi = lax.axis_index("gx")
    gyi = lax.axis_index("gy")
    nx = lax.axis_size("gx")
    ny = lax.axis_size("gy")
    xs = gxi * width_x - 1 + lax.broadcasted_iota(jnp.int32, (ext_x, ext_y), 0)
    ys = gyi * width_y - 1 + lax.broadcasted_iota(jnp.int32, (ext_x, ext_y), 1)
    in_grid = (xs >= 0) & (xs < nx * width_x) & (ys >= 0) & (ys < ny * width_y)
    first = jnp.where(in_grid, first[:, :, :ext_x, :ext_y], 0.0)
    term_one = term_ext[1 : 1 + width_x, 1 : 1 + width_y]
    pulled = pull_back(first, width_x, width_y)
    adjoint, term_two = adjoint_step(0, pulled, forward_pops, blocking, lever)
    raw = SENSE_SCALE * (term_one + term_two)
    smooth = helmholtz(raw, SWEEPS)
    region_one = (region_label == 1).astype(jnp.float32)
    region_two = (region_label == 2).astype(jnp.float32)
    stats = jnp.stack(
        [
            jnp.sum(smooth * region_one),
            jnp.sum(smooth * region_two),
            jnp.sum(region_one),
            jnp.sum(region_two),
        ]
    )
    stats = global_sum(stats)
    means = stats[:2] / jnp.maximum(stats[2:], 1.0)
    sensitivity = region_one * (smooth - means[0]) + region_two * (smooth - means[1])
    return (adjoint, sensitivity)


def solution(mesh):
    in_specs = (
        P(None, None, "gx", "gy"),
        P(None, None, None, "gx", "gy"),
        P(None, "gx", "gy"),
        P("gx", "gy"),
        P("gx", "gy"),
    )
    out_specs = (P(None, None, "gx", "gy"), P("gx", "gy"))
    return jax.shard_map(
        per_device, mesh=mesh, in_specs=in_specs, out_specs=out_specs, check_vma=False
    )
```

```python
import jax
import jax.numpy as jnp
from jax import lax
from jax.sharding import PartitionSpec as P

SWEEPS = 4


VELOCITIES = [
    (0, 0, 0),
    (1, 0, 0),
    (-1, 0, 0),
    (0, 1, 0),
    (0, -1, 0),
    (0, 0, 1),
    (0, 0, -1),
    (1, 1, 0),
    (-1, -1, 0),
    (1, -1, 0),
    (-1, 1, 0),
    (1, 0, 1),
    (-1, 0, -1),
    (1, 0, -1),
    (-1, 0, 1),
    (0, 1, 1),
    (0, -1, -1),
    (0, 1, -1),
    (0, -1, 1),
]
OPPOSITE = [0, 2, 1, 4, 3, 6, 5, 8, 7, 10, 9, 12, 11, 14, 13, 16, 15, 18, 17]
WEIGHTS = [1.0 / 3.0] + [1.0 / 18.0] * 6 + [1.0 / 36.0] * 12
RELAX_RATES = [0.0] * 4 + [1.6] * 6 + [1.4] * 6 + [1.2] * 3
EXPONENTS = [
    (0, 0, 0),
    (1, 0, 0),
    (0, 1, 0),
    (0, 0, 1),
    (2, 0, 0),
    (0, 2, 0),
    (0, 0, 2),
    (1, 1, 0),
    (1, 0, 1),
    (0, 1, 1),
    (2, 1, 0),
    (2, 0, 1),
    (1, 2, 0),
    (0, 2, 1),
    (1, 0, 2),
    (0, 1, 2),
    (2, 2, 0),
    (2, 0, 2),
    (0, 2, 2),
]
BLOCK_LIMIT = 0.5
SENSE_SCALE = 20.0
FILTER_WEIGHT = 16.0

import functools

from jax.experimental import pallas as pl
from jax.experimental.pallas import tpu as pltpu

def moment_table():
    rows_out = []
    for expo in EXPONENTS:
        vector = [
            float(vel[0] ** expo[0] * vel[1] ** expo[1] * vel[2] ** expo[2]) for vel in VELOCITIES
        ]
        for prior in rows_out:
            factor = sum((a * b for a, b in zip(vector, prior))) / sum((b * b for b in prior))
            vector = [a - factor * b for a, b in zip(vector, prior)]
        rows_out.append(vector)
    norms = [sum((b * b for b in row)) for row in rows_out]
    table = []
    for first in range(19):
        line = []
        for second in range(19):
            line.append(
                sum(
                    (
                        rows_out[k][first] / norms[k] * RELAX_RATES[k] * rows_out[k][second]
                        for k in range(19)
                    )
                )
            )
        table.append(line)
    return table


RELAX = moment_table()


def relax_groups():
    rows = []
    for line in RELAX:
        groups = []
        for l, value in enumerate(line):
            for group in groups:
                if abs(group[0] - value) <= 1e-12 * max(1.0, abs(value)):
                    group[1].append(l)
                    break
            else:
                groups.append((value, [l]))
        rows.append(groups)
    return rows


RELAX_GROUPS = relax_groups()


def halo(cells, w):
    return halo_many([cells], [w])[0]


def halo_many(arrays, widths):
    for axis, dim in (("gx", -2), ("gy", -1)):
        count = lax.axis_size(axis)
        heads, tails = [], []
        for a, w in zip(arrays, widths):
            size = a.shape[dim]
            heads.append(lax.slice_in_dim(a, 0, w, axis=a.ndim + dim))
            tails.append(lax.slice_in_dim(a, size - w, size, axis=a.ndim + dim))

        def send(pieces, pairs):
            if len(pieces) == 1:
                got = lax.ppermute(pieces[0].astype(jnp.float32), axis, pairs)
                return [got.astype(pieces[0].dtype)]
            flat = jnp.concatenate([p.astype(jnp.float32).reshape(-1) for p in pieces])
            got = lax.ppermute(flat, axis, pairs)
            out, at = [], 0
            for p in pieces:
                out.append(got[at : at + p.size].reshape(p.shape).astype(p.dtype))
                at += p.size
            return out

        lows = send(tails, [(i, i + 1) for i in range(count - 1)])
        highs = send(heads, [(i + 1, i) for i in range(count - 1)])
        arrays = [jnp.concatenate([lo, a, hi], axis=dim) for lo, a, hi in zip(lows, arrays, highs)]
    return arrays


def global_sum(values):
    axes = ("gx", "gy")
    count = lax.axis_size("gx") * lax.axis_size("gy")
    rows = jnp.broadcast_to(values[None, :], (count,) + values.shape)
    return jnp.sum(lax.all_to_all(rows, axes, 0, 0, tiled=True), axis=0)


def pull_back(ext, width_x, width_y):
    pieces = []
    for slot in range(19):
        step_x, step_y, step_z = VELOCITIES[slot]
        piece = ext[slot, :, 1 + step_x : 1 + step_x + width_x, 1 + step_y : 1 + step_y + width_y]
        pieces.append(jnp.roll(piece, -step_z, axis=0))
    return jnp.stack(pieces)


def cell_math(g, f, b, lev):
    rho = f[0]
    for i in range(1, 19):
        rho = rho + f[i]
    mom = []
    for d in range(3):
        acc = None
        for i in range(19):
            c = VELOCITIES[i][d]
            if c == 0:
                continue
            acc = (f[i] if acc is None else acc + f[i]) if c > 0 else (-f[i] if acc is None else acc - f[i])
        mom.append(acc)
    u = [m / rho for m in mom]
    usq = u[0] * u[0] + u[1] * u[1] + u[2] * u[2]
    one_b = 1.0 - b
    q = []
    for j in range(19):
        acc = None
        for value, members in RELAX_GROUPS[j]:
            part = g[members[0]]
            for l in members[1:]:
                part = part + g[l]
            t = value * part
            acc = t if acc is None else acc + t
        q.append(acc)
    tsum = None
    for i in range(19):
        cu = None
        for d in range(3):
            c = VELOCITIES[i][d]
            if c == 0:
                continue
            cu = (u[d] if c > 0 else -u[d]) if cu is None else (cu + u[d] if c > 0 else cu - u[d])
        if cu is None:
            phi = 1.0 - 1.5 * usq
        else:
            phi = 1.0 + 3.0 * cu + 4.5 * cu * cu - 1.5 * usq
        eq = WEIGHTS[i] * rho * phi
        t = g[i] * (f[OPPOSITE[i]] - f[i]) + q[i] * (f[i] - eq)
        tsum = t if tsum is None else tsum + t
    term = lev * tsum
    k = [one_b * qj for qj in q]
    wk = [WEIGHTS[i] * k[i] for i in range(19)]
    a_sum = wk[0]
    for i in range(1, 19):
        a_sum = a_sum + wk[i]
    bvec = []
    for d in range(3):
        acc = None
        for i in range(19):
            c = VELOCITIES[i][d]
            if c == 0:
                continue
            acc = (wk[i] if acc is None else acc + wk[i]) if c > 0 else (-wk[i] if acc is None else acc - wk[i])
        bvec.append(acc)
    cmat = {}
    for d in range(3):
        for e in range(d, 3):
            acc = None
            for i in range(19):
                c = VELOCITIES[i][d] * VELOCITIES[i][e]
                if c == 0:
                    continue
                acc = (wk[i] if acc is None else acc + wk[i]) if c > 0 else (-wk[i] if acc is None else acc - wk[i])
            cmat[(d, e)] = acc
            cmat[(e, d)] = acc
    cu_vec = [cmat[(d, 0)] * u[0] + cmat[(d, 1)] * u[1] + cmat[(d, 2)] * u[2] for d in range(3)]
    ucu = u[0] * cu_vec[0] + u[1] * cu_vec[1] + u[2] * cu_vec[2]
    e_val = a_sum - 4.5 * ucu + 1.5 * a_sum * usq
    gvec = [3.0 * bvec[d] + 9.0 * cu_vec[d] - 3.0 * a_sum * u[d] for d in range(3)]
    result = []
    for j in range(19):
        r = one_b * g[j] - k[j] + e_val + b * g[OPPOSITE[j]]
        for d in range(3):
            c = VELOCITIES[j][d]
            if c > 0:
                r = r + gvec[d]
            elif c < 0:
                r = r - gvec[d]
        result.append(r)
    return result, term


def step_kernel(section, rows, g_ref, f_ref, b_ref, l_ref, res_ref, term_ref):
    planes, width_x, _ = b_ref.shape
    chunks = width_x // rows

    def body(idx, acc):
        z = idx // chunks
        x0 = pl.multiple_of((idx % chunks) * rows, rows)
        xs = pl.ds(x0, rows)
        g = [g_ref[i, z, xs, :] for i in range(19)]
        f = [f_ref[section, i, z, xs, :].astype(jnp.float32) for i in range(19)]
        b = b_ref[z, xs, :]
        lev = l_ref[z, xs, :]
        result, term = cell_math(g, f, b, lev)
        for j in range(19):
            res_ref[j, z, xs, :] = result[j]
        term_ref[xs, :] = term_ref[xs, :] + term
        return acc

    term_ref[...] = jnp.zeros_like(term_ref)
    lax.fori_loop(0, planes * chunks, body, 0)


def adjoint_step(section, pulled, forward_pops, blocking, lever):
    planes, width_x, width_y = blocking.shape
    rows = max(8, 2048 // width_y)
    if width_x % rows:
        rows = 8 if width_x % 8 == 0 else width_x
    vmem = pl.BlockSpec(memory_space=pltpu.VMEM)
    return pl.pallas_call(
        functools.partial(step_kernel, section, rows),
        out_shape=(
            jax.ShapeDtypeStruct((19, planes, width_x, width_y), jnp.float32),
            jax.ShapeDtypeStruct((width_x, width_y), jnp.float32),
        ),
        in_specs=[vmem] * 4,
        out_specs=(vmem, vmem),
    )(pulled, forward_pops, blocking, lever)


def helmholtz(raw, w):
    scale_den = 1.0 + 4.0 * FILTER_WEIGHT
    width_x, width_y = raw.shape
    nx = lax.axis_size("gx")
    ny = lax.axis_size("gy")
    gxi = lax.axis_index("gx")
    gyi = lax.axis_index("gy")
    raw_ext = halo(raw, w)
    xs = gxi * width_x - w + lax.broadcasted_iota(jnp.int32, raw_ext.shape, 0)
    ys = gyi * width_y - w + lax.broadcasted_iota(jnp.int32, raw_ext.shape, 1)
    valid = (xs >= 0) & (xs < nx * width_x) & (ys >= 0) & (ys < ny * width_y)
    smooth = raw_ext
    for sweep in range(SWEEPS):
        framed = jnp.pad(smooth, 1)
        beside_all = framed[:-2, 1:-1] + framed[2:, 1:-1] + framed[1:-1, :-2] + framed[1:-1, 2:]
        smooth = jnp.where(valid, (raw_ext + FILTER_WEIGHT * beside_all) / scale_den, 0.0)
    return smooth[w:-w, w:-w]


def pad_to(a, rows, cols):
    pad = [(0, 0)] * (a.ndim - 2) + [(0, rows - a.shape[-2]), (0, cols - a.shape[-1])]
    return jnp.pad(a, pad)


def per_device(adjoint_in, forward_pops, solid_mask, region_label, design):
    planes, width_x, width_y = solid_mask.shape
    inside = region_label > 0
    blocking = jnp.where(
        solid_mask == 1, 1.0, jnp.where(inside[None], BLOCK_LIMIT * design[None], 0.0)
    ).astype(jnp.float32)
    lever = jnp.where((solid_mask == 0) & inside[None], BLOCK_LIMIT, 0.0).astype(jnp.float32)
    saved_one = forward_pops[1]
    adj_ext, saved_ext, solid_ext, label_ext, design_ext = halo_many(
        [adjoint_in, saved_one, solid_mask, region_label, design], [2, 1, 1, 1, 1]
    )
    block_ext = jnp.where(
        solid_ext == 1, 1.0, jnp.where((label_ext > 0)[None], BLOCK_LIMIT * design_ext[None], 0.0)
    ).astype(jnp.float32)
    ext_x, ext_y = width_x + 2, width_y + 2
    rows = -(-ext_x // 8) * 8
    cols = -(-ext_y // 128) * 128
    pulled = pad_to(pull_back(adj_ext, ext_x, ext_y), rows, cols)
    first, term_ext = adjoint_step(
        0,
        pulled,
        pad_to(saved_ext, rows, cols)[None],
        pad_to(block_ext, rows, cols),
        pad_to(jnp.pad(lever, ((0, 0), (1, 1), (1, 1))), rows, cols),
    )
    gxi = lax.axis_index("gx")
    gyi = lax.axis_index("gy")
    nx = lax.axis_size("gx")
    ny = lax.axis_size("gy")
    xs = gxi * width_x - 1 + lax.broadcasted_iota(jnp.int32, (ext_x, ext_y), 0)
    ys = gyi * width_y - 1 + lax.broadcasted_iota(jnp.int32, (ext_x, ext_y), 1)
    in_grid = (xs >= 0) & (xs < nx * width_x) & (ys >= 0) & (ys < ny * width_y)
    first = jnp.where(in_grid, first[:, :, :ext_x, :ext_y], 0.0)
    term_one = term_ext[1 : 1 + width_x, 1 : 1 + width_y]
    pulled = pull_back(first, width_x, width_y)
    adjoint, term_two = adjoint_step(0, pulled, forward_pops, blocking, lever)
    raw = SENSE_SCALE * (term_one + term_two)
    smooth = helmholtz(raw, SWEEPS)
    region_one = (region_label == 1).astype(jnp.float32)
    region_two = (region_label == 2).astype(jnp.float32)
    stats = jnp.stack(
        [
            jnp.sum(smooth * region_one),
            jnp.sum(smooth * region_two),
            jnp.sum(region_one),
            jnp.sum(region_two),
        ]
    )
    stats = global_sum(stats)
    means = stats[:2] / jnp.maximum(stats[2:], 1.0)
    sensitivity = region_one * (smooth - means[0]) + region_two * (smooth - means[1])
    return (adjoint, sensitivity)


def solution(mesh):
    in_specs = (
        P(None, None, "gx", "gy"),
        P(None, None, None, "gx", "gy"),
        P(None, "gx", "gy"),
        P("gx", "gy"),
        P("gx", "gy"),
    )
    out_specs = (P(None, None, "gx", "gy"), P("gx", "gy"))
    return jax.shard_map(
        per_device, mesh=mesh, in_specs=in_specs, out_specs=out_specs, check_vma=False
    )
```
